32 devices in a mesh: rows: 8 (over z, y), sub: 4 (over x, core).
Axes of the slice: x: 2, y: 2, z: 4, core: 2. Of those that a mesh axis runs over, the one named last changes fastest.
Arguments:
- held: float32 [512, 4, 128, 256], P('rows', 'sub'), may hold values from -256 to 256
- held_block: int32 [512, 4], P('rows', 'sub'), may hold values from 0 to 255, as said below
- held_count: int32 [8, 4], P('rows', 'sub'), may hold values from 0 to 64
Outputs:
- q_factor: float32 [256, 4, 128, 256], P('rows', 'sub')
- r_factor: float32 [256, 256], replicated
The draws below stay inside these ranges and needn't reach their ends.
Inputs may be any that keep to these rules, and one draw needn't show every extreme that they name: `held_block`: for slots j < held_count of a device, the ids are block numbers of its column group; over all devices of a column group each block is held in exactly one such slot. Slots at or past held_count hold arbitrary ids and data. A device holds at most 8 blocks whose number b has b // 32 equal to any one given device index along rows, and some device reaches that.
All inputs are finite; a program needn't handle non-finite values.
Results may differ from the reference program's by a relative error of at most 0.0003.
Values sent between devices are 32-bit elements; how exact they have to be, the bound alone decides.
No kernel may reach another device: no remote copies, remote signals or barrier semaphores. Data moves between devices by JAX's collectives and lax.ppermute only.
A program may use at most 128 MiB of HBM per device.

```python
import math
import jax
import jax.numpy as jnp
from jax import lax

W = 256
BLOCK = 128
BLK_DEV = 32
CAP = 64
NB_COL = 256
ROWS_ALL = 131072
N_ROWS = 8
N_SUB = 4


def layout(key):
    pair_key = jax.random.fold_in(key, 11)
    pick_key = jax.random.fold_in(key, 12)
    junk_key = jax.random.fold_in(key, 13)
    pairs = N_ROWS // 2
    share = jax.random.randint(pair_key, (N_SUB, pairs), 0, CAP + 1)
    forced = jax.random.randint(pick_key, (N_SUB, 1), 0, pairs)
    share = jnp.where(jnp.arange(pairs)[None, :] == forced, 0, share)
    counts = jnp.stack([share, CAP - share], axis=2).reshape(N_SUB, N_ROWS)
    starts = jnp.cumsum(counts, axis=1) - counts
    slots = jnp.arange(CAP)
    position = starts[:, :, None] + slots[None, None, :]
    valid = slots[None, None, :] < counts[:, :, None]
    junk = jax.random.randint(junk_key, position.shape, 0, NB_COL)
    position = jnp.where(valid, position, junk)
    block_id = position % N_ROWS * BLK_DEV + position // N_ROWS
    return (block_id, counts)


def draw_held_block(key, part):
    block_id, counts = layout(key)
    return jnp.transpose(block_id, (1, 2, 0)).reshape(N_ROWS * CAP, N_SUB).astype(jnp.int32)


def draw_held_count(key, part):
    block_id, counts = layout(key)
    return counts.T.astype(jnp.int32)


def draw_held(key, part):
    block_id, counts = layout(key)
    block_ids = jnp.transpose(block_id, (1, 2, 0)).reshape(N_ROWS * CAP, N_SUB)
    trend = 0.5 + block_ids.astype(jnp.float32) / NB_COL
    row_shape = (N_ROWS * CAP, N_SUB, BLOCK)
    shape = (N_ROWS * CAP, N_SUB, BLOCK, W)
    row_scale = jnp.exp(jax.random.uniform(jax.random.fold_in(key, 21), row_shape, jnp.float32, math.log(0.32), math.log(3.2)))
    col_scale = jnp.exp(jax.random.uniform(jax.random.fold_in(key, 22), (W,), jnp.float32, math.log(0.32), math.log(3.2)))
    noise = jnp.clip(jax.random.normal(jax.random.fold_in(key, 23), shape, jnp.float32), -4.0, 4.0)
    mode_one = jnp.clip(jax.random.normal(jax.random.fold_in(key, 24), row_shape, jnp.float32), -4.0, 4.0)
    mode_two = jnp.clip(jax.random.normal(jax.random.fold_in(key, 26), row_shape, jnp.float32), -4.0, 4.0)
    mode_three = jnp.clip(jax.random.normal(jax.random.fold_in(key, 27), row_shape, jnp.float32), -4.0, 4.0)
    loading_one = jax.random.uniform(jax.random.fold_in(key, 25), (W,), jnp.float32, 0.5, 1.5)
    loading_two = jax.random.uniform(jax.random.fold_in(key, 28), (W,), jnp.float32, -1.0, 1.0)
    loading_three = jax.random.uniform(jax.random.fold_in(key, 29), (W,), jnp.float32, -1.0, 1.0)
    banded = noise + 0.8 * jnp.roll(noise, 1, axis=3) + 0.5 * jnp.roll(noise, 2, axis=3)
    base = mode_one[..., None] * loading_one + 0.6 * mode_two[..., None] * loading_two
    base = base + 0.35 * mode_three[..., None] * loading_three + 0.25 * banded
    return base * row_scale[..., None] * trend[:, :, None, None] * col_scale


def setup_inputs(seed: int = 0) -> dict:
    streams_of = jax.random.split(jax.random.key(seed), 4)
    held = draw_held(jax.random.fold_in(streams_of[3], 71), 0)
    held_block = draw_held_block(jax.random.fold_in(streams_of[3], 71), 0)
    held_count = draw_held_count(jax.random.fold_in(streams_of[3], 71), 0)
    return dict(held=held, held_block=held_block, held_count=held_count)


def factor(gram):
    lower = jnp.linalg.cholesky(gram)
    identity = jnp.eye(gram.shape[0], dtype=gram.dtype)
    inverse = lax.linalg.triangular_solve(lower, identity, left_side=True, lower=True)
    return (lower, inverse)

def gram_of(flattened, total):
    return lax.dot_general(flattened.astype(jnp.float32), flattened.astype(jnp.float32), (((0,), (0,)), ((), ())), precision=lax.Precision.HIGHEST, preferred_element_type=jnp.float32) / total

def apply_inverse(flattened, inverse):
    return jnp.dot(flattened.astype(jnp.float32), inverse.T.astype(jnp.float32), precision=lax.Precision.HIGHEST, preferred_element_type=jnp.float32)

def reference(held, held_block, held_count):
    data = held.reshape(N_ROWS, CAP, N_SUB, BLOCK, W)
    block_ids = held_block.reshape(N_ROWS, CAP, N_SUB)
    slots = jnp.arange(CAP, dtype=jnp.int32)
    valid = slots[None, :, None] < held_count[:, None, :]
    target = jnp.where(valid, block_ids, NB_COL).astype(jnp.int32)
    column = jnp.broadcast_to(jnp.arange(N_SUB, dtype=jnp.int32)[None, None, :], target.shape)
    snapshots = jnp.zeros((N_SUB, NB_COL, BLOCK, W), held.dtype).at[column, target].set(data, mode='drop')
    flattened = snapshots.reshape(-1, W)
    total = float(ROWS_ALL)
    lower_one, inverse_one = factor(gram_of(flattened, total))
    first = apply_inverse(flattened, inverse_one)
    lower_two, inverse_two = factor(gram_of(first, total))
    second = apply_inverse(first, inverse_two)
    q_factor = second.reshape(N_SUB, NB_COL, BLOCK, W).transpose(1, 0, 2, 3)
    r_factor = jnp.dot(lower_two.T.astype(jnp.float32), lower_one.T.astype(jnp.float32), precision=lax.Precision.HIGHEST, preferred_element_type=jnp.float32)
    return (q_factor, r_factor)
```

```python
import jax
import jax.numpy as jnp
from jax import lax
from jax.sharding import PartitionSpec as P

BLK_DEV = 32


def factor(gram):
    lower = jnp.linalg.cholesky(gram)
    identity = jnp.eye(gram.shape[0], dtype=gram.dtype)
    inverse = lax.linalg.triangular_solve(lower, identity, left_side=True, lower=True)
    return (lower, inverse)


def gram_of(flattened, total):
    return (
        lax.dot_general(
            flattened,
            flattened,
            (((0,), (0,)), ((), ())),
            precision=lax.Precision.HIGHEST,
            preferred_element_type=jnp.float32,
        )
        / total
    )


def apply_inverse(flattened, inverse):
    return jnp.dot(
        flattened, inverse.T, precision=lax.Precision.HIGHEST, preferred_element_type=jnp.float32
    )


def _xor_pairs(n, bit):
    return [(i, i ^ bit) for i in range(n)]


def _power_of_two(n):
    return n > 0 and (n & (n - 1)) == 0


def reduce_gram(partial_value):
    n_sub = lax.axis_size("sub")
    n_rows = lax.axis_size("rows")
    width = partial_value.shape[0]
    if not (_power_of_two(n_sub) and _power_of_two(n_rows) and n_sub >= 2 and width % 2 == 0):
        return lax.psum(partial_value, ("rows", "sub"))
    x = partial_value + lax.ppermute(partial_value, "sub", _xor_pairs(n_sub, 1))
    half = width // 2
    h = lax.axis_index("sub") % 2
    y = lax.dynamic_slice_in_dim(x, h * half, half, 0)
    bit = 2
    while bit < n_sub:
        y = y + lax.ppermute(y, "sub", _xor_pairs(n_sub, bit))
        bit *= 2
    bit = 1
    while bit < n_rows:
        y = y + lax.ppermute(y, "rows", _xor_pairs(n_rows, bit))
        bit *= 2
    other = lax.ppermute(y, "sub", _xor_pairs(n_sub, 1))
    first_half = jnp.where(h == 0, y, other)
    second_half = jnp.where(h == 0, other, y)
    return jnp.concatenate([first_half, second_half], axis=0)


def per_device(held, held_block, held_count):
    capacity = held.shape[0]
    block_rows = held.shape[2]
    width = held.shape[3]
    devices_rows = lax.axis_size("rows")
    own_index = lax.axis_index("rows")
    per_slot = max(1, capacity // devices_rows)
    n_out = devices_rows * per_slot
    total = float(devices_rows * lax.axis_size("sub") * BLK_DEV * block_rows)
    blocks = held[:, 0]
    block_ids = held_block[:, 0]
    count = held_count[0, 0]
    slots = jnp.arange(capacity, dtype=jnp.int32)
    valid = slots < count

    destination = block_ids // BLK_DEV
    earlier = (
        (destination[:, None] == destination[None, :])
        & valid[None, :]
        & (slots[None, :] < slots[:, None])
    )
    rank_within = jnp.sum(earlier.astype(jnp.int32), axis=1)
    target = jnp.where(valid, destination * per_slot + rank_within, n_out)
    positions = jnp.arange(n_out, dtype=jnp.int32)
    match = target[None, :] == positions[:, None]
    source = jnp.sum(jnp.where(match, slots[None, :], 0), axis=1)
    present = jnp.any(match, axis=1)
    labels = jnp.where(present, jnp.take(block_ids, source), -1).astype(jnp.int32)
    outgoing = jnp.take(blocks, source, axis=0)
    arrived = lax.all_to_all(outgoing, "rows", split_axis=0, concat_axis=0, tiled=True)
    arrived_labels = lax.all_to_all(labels, "rows", split_axis=0, concat_axis=0, tiled=True)

    masked = jnp.where(valid[:, None, None], blocks, 0.0).reshape(-1, width)
    lower_one, inverse_one = factor(reduce_gram(gram_of(masked, total)))
    first_held = apply_inverse(masked, inverse_one)
    lower_two, inverse_two = factor(reduce_gram(gram_of(first_held, total)))

    wanted = own_index * BLK_DEV + jnp.arange(BLK_DEV, dtype=jnp.int32)
    hit = arrived_labels[None, :] == wanted[:, None]
    place = jnp.sum(jnp.where(hit, positions[None, :], 0), axis=1)
    resident = jnp.take(arrived, place, axis=0).reshape(-1, width)
    first = apply_inverse(resident, inverse_one)
    second = apply_inverse(first, inverse_two)
    result = second.reshape(BLK_DEV, block_rows, width)
    r_factor = jnp.dot(
        lower_two.T,
        lower_one.T,
        precision=lax.Precision.HIGHEST,
        preferred_element_type=jnp.float32,
    )
    return (result[:, None], r_factor)


def solution(mesh):
    in_specs = (P("rows", "sub", None, None), P("rows", "sub"), P("rows", "sub"))
    out_specs = (P("rows", "sub", None, None), P())
    return jax.shard_map(
        per_device, mesh=mesh, in_specs=in_specs, out_specs=out_specs, check_vma=False
    )
```

```python
import jax
import jax.numpy as jnp
from jax import lax
from jax.sharding import PartitionSpec as P

BLK_DEV = 32


def factor(gram):
    lower = jnp.linalg.cholesky(gram)
    identity = jnp.eye(gram.shape[0], dtype=gram.dtype)
    inverse = lax.linalg.triangular_solve(lower, identity, left_side=True, lower=True)
    return (lower, inverse)


def gram_of(flattened, total):
    return (
        lax.dot_general(
            flattened,
            flattened,
            (((0,), (0,)), ((), ())),
            precision=lax.Precision.HIGHEST,
            preferred_element_type=jnp.float32,
        )
        / total
    )


def apply_inverse(flattened, inverse):
    return jnp.dot(
        flattened, inverse.T, precision=lax.Precision.HIGHEST, preferred_element_type=jnp.float32
    )


def _xor_pairs(n, bit):
    return [(i, i ^ bit) for i in range(n)]


def _power_of_two(n):
    return n > 0 and (n & (n - 1)) == 0


def reduce_gram(partial_value):
    n_sub = lax.axis_size("sub")
    n_rows = lax.axis_size("rows")
    width = partial_value.shape[0]
    if not (_power_of_two(n_sub) and _power_of_two(n_rows) and n_sub >= 2 and width % 2 == 0):
        return lax.psum(partial_value, ("rows", "sub"))
    x = partial_value + lax.ppermute(partial_value, "sub", _xor_pairs(n_sub, 1))
    half = width // 2
    h = lax.axis_index("sub") % 2
    y = lax.dynamic_slice_in_dim(x, h * half, half, 0)
    bit = 2
    while bit < n_sub:
        y = y + lax.ppermute(y, "sub", _xor_pairs(n_sub, bit))
        bit *= 2
    bit = 1
    while bit < n_rows:
        y = y + lax.ppermute(y, "rows", _xor_pairs(n_rows, bit))
        bit *= 2
    other = lax.ppermute(y, "sub", _xor_pairs(n_sub, 1))
    first_half = jnp.where(h == 0, y, other)
    second_half = jnp.where(h == 0, other, y)
    return jnp.concatenate([first_half, second_half], axis=0)


def per_device(held, held_block, held_count):
    capacity = held.shape[0]
    block_rows = held.shape[2]
    width = held.shape[3]
    devices_rows = lax.axis_size("rows")
    own_index = lax.axis_index("rows")
    per_slot = max(1, capacity // devices_rows)
    n_out = devices_rows * per_slot
    total = float(devices_rows * lax.axis_size("sub") * BLK_DEV * block_rows)
    blocks = held[:, 0]
    block_ids = held_block[:, 0]
    count = held_count[0, 0]
    slots = jnp.arange(capacity, dtype=jnp.int32)
    valid = slots < count

    destination = block_ids // BLK_DEV
    earlier = (
        (destination[:, None] == destination[None, :])
        & valid[None, :]
        & (slots[None, :] < slots[:, None])
    )
    rank_within = jnp.sum(earlier.astype(jnp.int32), axis=1)
    target = jnp.where(valid, destination * per_slot + rank_within, n_out)
    positions = jnp.arange(n_out, dtype=jnp.int32)
    match = target[None, :] == positions[:, None]
    source = jnp.sum(jnp.where(match, slots[None, :], 0), axis=1)
    present = jnp.any(match, axis=1)
    labels = jnp.where(present, jnp.take(block_ids, source), -1).astype(jnp.int32)
    arrived_labels = lax.all_to_all(labels, "rows", split_axis=0, concat_axis=0, tiled=True)
    source = source.reshape(devices_rows, per_slot)

    early = per_slot // 8
    middle = per_slot // 2
    bounds = [(0, early), (early, early + middle), (early + middle, per_slot)]

    def send(lo, hi, after):
        if hi <= lo:
            return None
        chunk_source = source[:, lo:hi].reshape(-1)
        if after is not None:
            chunk_source, _ = lax.optimization_barrier((chunk_source, after))
        outgoing = jnp.take(blocks, chunk_source, axis=0)
        return lax.all_to_all(outgoing, "rows", split_axis=0, concat_axis=0, tiled=True)

    def settle(value, chunk):
        if chunk is None:
            return value
        value, _ = lax.optimization_barrier((value, chunk))
        return value

    arrived = [None, None, None]
    masked = jnp.where(valid[:, None, None], blocks, 0.0).reshape(-1, width)
    arrived[0] = send(*bounds[0], None)
    gram_one = settle(gram_of(masked, total), arrived[0])
    reduced_one = reduce_gram(gram_one)
    arrived[1] = send(*bounds[1], reduced_one)
    lower_one, inverse_one = factor(reduced_one)
    first_held = apply_inverse(masked, inverse_one)
    gram_two = settle(gram_of(first_held, total), arrived[1])
    reduced_two = reduce_gram(gram_two)
    arrived[2] = send(*bounds[2], reduced_two)
    lower_two, inverse_two = factor(reduced_two)

    pieces = []
    piece_labels = []
    for (lo, hi), chunk in zip(bounds, arrived):
        if chunk is None:
            continue
        pieces.append(chunk)
        piece_labels.append(arrived_labels.reshape(devices_rows, per_slot)[:, lo:hi].reshape(-1))
    all_arrived = jnp.concatenate(pieces, axis=0)
    all_labels = jnp.concatenate(piece_labels, axis=0)
    wanted = own_index * BLK_DEV + jnp.arange(BLK_DEV, dtype=jnp.int32)
    hit = all_labels[None, :] == wanted[:, None]
    place = jnp.sum(jnp.where(hit, positions[None, :], 0), axis=1)
    resident = jnp.take(all_arrived, place, axis=0).reshape(-1, width)
    first = apply_inverse(resident, inverse_one)
    second = apply_inverse(first, inverse_two)
    result = second.reshape(BLK_DEV, block_rows, width)
    r_factor = jnp.dot(
        lower_two.T,
        lower_one.T,
        precision=lax.Precision.HIGHEST,
        preferred_element_type=jnp.float32,
    )
    return (result[:, None], r_factor)


def solution(mesh):
    in_specs = (P("rows", "sub", None, None), P("rows", "sub"), P("rows", "sub"))
    out_specs = (P("rows", "sub", None, None), P())
    return jax.shard_map(
        per_device, mesh=mesh, in_specs=in_specs, out_specs=out_specs, check_vma=False
    )
```

```python
import jax
import jax.numpy as jnp
from jax import lax
from jax.sharding import PartitionSpec as P

BLK_DEV = 32


def factor(gram):
    lower = jnp.linalg.cholesky(gram)
    identity = jnp.eye(gram.shape[0], dtype=gram.dtype)
    inverse = lax.linalg.triangular_solve(lower, identity, left_side=True, lower=True)
    return (lower, inverse)


def gram_of(flattened, total):
    return (
        lax.dot_general(
            flattened,
            flattened,
            (((0,), (0,)), ((), ())),
            precision=lax.Precision.HIGHEST,
            preferred_element_type=jnp.float32,
        )
        / total
    )


def apply_inverse(flattened, inverse):
    return jnp.dot(
        flattened, inverse.T, precision=lax.Precision.HIGHEST, preferred_element_type=jnp.float32
    )


def _xor_pairs(n, bit):
    return [(i, i ^ bit) for i in range(n)]


def _power_of_two(n):
    return n > 0 and (n & (n - 1)) == 0


def reduce_gram(partial_value):
    n_sub = lax.axis_size("sub")
    n_rows = lax.axis_size("rows")
    width = partial_value.shape[0]
    if not (_power_of_two(n_sub) and _power_of_two(n_rows) and n_sub >= 2 and width % 2 == 0):
        return lax.psum(partial_value, ("rows", "sub"))
    x = partial_value + lax.ppermute(partial_value, "sub", _xor_pairs(n_sub, 1))
    half = width // 2
    h = lax.axis_index("sub") % 2
    y = lax.dynamic_slice_in_dim(x, h * half, half, 0)
    bit = 2
    while bit < n_sub:
        y = y + lax.ppermute(y, "sub", _xor_pairs(n_sub, bit))
        bit *= 2
    bit = 1
    while bit < n_rows:
        y = y + lax.ppermute(y, "rows", _xor_pairs(n_rows, bit))
        bit *= 2
    other = lax.ppermute(y, "sub", _xor_pairs(n_sub, 1))
    first_half = jnp.where(h == 0, y, other)
    second_half = jnp.where(h == 0, other, y)
    return jnp.concatenate([first_half, second_half], axis=0)


def per_device(held, held_block, held_count):
    capacity = held.shape[0]
    block_rows = held.shape[2]
    width = held.shape[3]
    devices_rows = lax.axis_size("rows")
    own_index = lax.axis_index("rows")
    per_slot = max(1, capacity // devices_rows)
    n_out = devices_rows * per_slot
    total = float(devices_rows * lax.axis_size("sub") * BLK_DEV * block_rows)
    blocks = held[:, 0]
    block_ids = held_block[:, 0]
    count = held_count[0, 0]
    slots = jnp.arange(capacity, dtype=jnp.int32)
    valid = slots < count

    def route(ids, filled):
        destination = ids // BLK_DEV
        earlier = (
            (destination[:, None] == destination[None, :])
            & filled[None, :]
            & (slots[None, :] < slots[:, None])
        )
        rank_within = jnp.sum(earlier.astype(jnp.int32), axis=1)
        return jnp.where(filled, destination * per_slot + rank_within, n_out)

    target = route(block_ids, valid)
    positions = jnp.arange(n_out, dtype=jnp.int32)
    match = target[None, :] == positions[:, None]
    source = jnp.sum(jnp.where(match, slots[None, :], 0), axis=1)
    source = source.reshape(devices_rows, per_slot)

    present = jnp.any(match, axis=1)
    labels = jnp.where(present, jnp.take(block_ids, jnp.sum(jnp.where(match, slots[None, :], 0), axis=1), mode="clip"), -1)
    labels = labels.reshape(devices_rows, per_slot).astype(jnp.float32)

    early = per_slot // 8
    middle = per_slot // 2
    bounds = [(0, early), (early, early + middle), (early + middle, per_slot)]

    def send(lo, hi, after, with_labels):
        if hi <= lo:
            return None, None
        chunk_source = source[:, lo:hi].reshape(-1)
        outgoing = jnp.take(blocks, chunk_source, axis=0, mode="clip")
        if with_labels:
            tile = jnp.zeros((devices_rows, 8, width), jnp.float32)
            tile = tile.at[:, 0, :per_slot].set(labels)
            outgoing = outgoing.reshape(devices_rows, (hi - lo) * block_rows, width)
            outgoing = jnp.concatenate([outgoing, tile], axis=1)
        if after is not None:
            outgoing, _ = lax.optimization_barrier((outgoing, after))
        arrived = lax.all_to_all(outgoing, "rows", split_axis=0, concat_axis=0, tiled=True)
        if not with_labels:
            return arrived, None
        got = arrived[:, (hi - lo) * block_rows, :per_slot].astype(jnp.int32)
        data = arrived[:, : (hi - lo) * block_rows].reshape(-1, block_rows, width)
        return data, got

    def settle(value, chunk):
        if chunk is None:
            return value
        value, _ = lax.optimization_barrier((value, chunk))
        return value

    def masked_gram(rows_of):
        kept = jnp.where(valid[:, None, None], rows_of.reshape(capacity, block_rows, width), 0.0)
        return (
            lax.dot_general(
                kept.reshape(-1, width),
                rows_of,
                (((0,), (0,)), ((), ())),
                precision=lax.Precision.HIGHEST,
                preferred_element_type=jnp.float32,
            )
            / total
        )

    arrived = [None, None, None]
    carrier = [k for k, (lo, hi) in enumerate(bounds) if hi > lo][0]
    flat = blocks.reshape(-1, width)
    arrived[0], got0 = send(*bounds[0], None, carrier == 0)
    gram_one = settle(masked_gram(flat), arrived[0])
    reduced_one = reduce_gram(gram_one)
    arrived[1], got1 = send(*bounds[1], reduced_one, carrier == 1)
    lower_one, inverse_one = factor(reduced_one)
    first_held = apply_inverse(flat, inverse_one)
    gram_two = settle(masked_gram(first_held), arrived[1])
    reduced_two = reduce_gram(gram_two)
    arrived[2], got2 = send(*bounds[2], reduced_two, carrier == 2)
    lower_two, inverse_two = factor(reduced_two)
    arrived_labels = [got0, got1, got2][carrier]

    pieces = []
    piece_labels = []
    for (lo, hi), chunk in zip(bounds, arrived):
        if chunk is None:
            continue
        pieces.append(chunk)
        piece_labels.append(arrived_labels[:, lo:hi].reshape(-1))
    all_arrived = jnp.concatenate(pieces, axis=0)
    all_labels = jnp.concatenate(piece_labels, axis=0)
    wanted = own_index * BLK_DEV + jnp.arange(BLK_DEV, dtype=jnp.int32)
    hit = all_labels[None, :] == wanted[:, None]
    place = jnp.sum(jnp.where(hit, positions[None, :], 0), axis=1)
    resident = jnp.take(all_arrived, place, axis=0, mode="clip").reshape(-1, width)
    first = apply_inverse(resident, inverse_one)
    second = apply_inverse(first, inverse_two)
    result = second.reshape(BLK_DEV, block_rows, width)
    r_factor = jnp.dot(
        lower_two.T,
        lower_one.T,
        precision=lax.Precision.HIGHEST,
        preferred_element_type=jnp.float32,
    )
    return (result[:, None], r_factor)


def solution(mesh):
    in_specs = (P("rows", "sub", None, None), P("rows", "sub"), P("rows", "sub"))
    out_specs = (P("rows", "sub", None, None), P())
    return jax.shard_map(
        per_device, mesh=mesh, in_specs=in_specs, out_specs=out_specs, check_vma=False
    )
```

```python
import jax
import jax.numpy as jnp
from jax import lax
from jax.sharding import PartitionSpec as P

BLK_DEV = 32


def _mm(a, b):
    return jnp.dot(a, b, precision=lax.Precision.HIGHEST, preferred_element_type=jnp.float32)


def _lower_inverse(lower):
    identity = jnp.eye(lower.shape[0], dtype=lower.dtype)
    return lax.linalg.triangular_solve(lower, identity, left_side=True, lower=True)


def factor(gram):
    n = gram.shape[0]
    if n % 2 or n < 256:
        lower = jnp.linalg.cholesky(gram)
        return (lower, _lower_inverse(lower))
    k = n // 2
    lower_11 = jnp.linalg.cholesky(gram[:k, :k])
    inverse_11 = _lower_inverse(lower_11)
    lower_21 = _mm(gram[k:, :k], inverse_11.T)
    lower_22 = jnp.linalg.cholesky(gram[k:, k:] - _mm(lower_21, lower_21.T))
    inverse_22 = _lower_inverse(lower_22)
    inverse_21 = -_mm(inverse_22, _mm(lower_21, inverse_11))
    zeros = jnp.zeros((k, n - k), gram.dtype)
    lower = jnp.block([[lower_11, zeros], [lower_21, lower_22]])
    inverse = jnp.block([[inverse_11, zeros], [inverse_21, inverse_22]])
    return (lower, inverse)


def gram_of(flattened, total):
    return (
        lax.dot_general(
            flattened,
            flattened,
            (((0,), (0,)), ((), ())),
            precision=lax.Precision.HIGHEST,
            preferred_element_type=jnp.float32,
        )
        / total
    )


def apply_inverse(flattened, inverse):
    return jnp.dot(
        flattened, inverse.T, precision=lax.Precision.HIGHEST, preferred_element_type=jnp.float32
    )


def _xor_pairs(n, bit):
    return [(i, i ^ bit) for i in range(n)]


def _power_of_two(n):
    return n > 0 and (n & (n - 1)) == 0


def reduce_gram(partial_value):
    n_sub = lax.axis_size("sub")
    n_rows = lax.axis_size("rows")
    width = partial_value.shape[0]
    if not (_power_of_two(n_sub) and _power_of_two(n_rows) and n_sub >= 2 and width % 2 == 0):
        return lax.psum(partial_value, ("rows", "sub"))
    x = partial_value + lax.ppermute(partial_value, "sub", _xor_pairs(n_sub, 1))
    half = width // 2
    h = lax.axis_index("sub") % 2
    y = lax.dynamic_slice_in_dim(x, h * half, half, 0)
    bit = 2
    while bit < n_sub:
        y = y + lax.ppermute(y, "sub", _xor_pairs(n_sub, bit))
        bit *= 2
    bit = 1
    while bit < n_rows:
        y = y + lax.ppermute(y, "rows", _xor_pairs(n_rows, bit))
        bit *= 2
    other = lax.ppermute(y, "sub", _xor_pairs(n_sub, 1))
    first_half = jnp.where(h == 0, y, other)
    second_half = jnp.where(h == 0, other, y)
    return jnp.concatenate([first_half, second_half], axis=0)


def _gate(value, deps):
    flag = jnp.zeros((), jnp.bool_)
    for dep in deps:
        if dep is None:
            continue
        probe = dep[(0,) * dep.ndim]
        flag = flag | (probe != probe)
    corner = value[(slice(0, 1),) * value.ndim]
    kept = jnp.where(flag, jnp.zeros_like(corner), corner)
    return lax.dynamic_update_slice(value, kept, (0,) * value.ndim)


def per_device(held, held_block, held_count):
    capacity = held.shape[0]
    block_rows = held.shape[2]
    width = held.shape[3]
    devices_rows = lax.axis_size("rows")
    own_index = lax.axis_index("rows")
    per_slot = max(1, capacity // devices_rows)
    n_out = devices_rows * per_slot
    total = float(devices_rows * lax.axis_size("sub") * BLK_DEV * block_rows)
    blocks = held[:, 0]
    block_ids = held_block[:, 0]
    count = held_count[0, 0]
    slots = jnp.arange(capacity, dtype=jnp.int32)
    valid = slots < count

    def route(ids, filled):
        destination = ids // BLK_DEV
        earlier = (
            (destination[:, None] == destination[None, :])
            & filled[None, :]
            & (slots[None, :] < slots[:, None])
        )
        rank_within = jnp.sum(earlier.astype(jnp.int32), axis=1)
        return jnp.where(filled, destination * per_slot + rank_within, n_out)

    target = route(block_ids, valid)
    positions = jnp.arange(n_out, dtype=jnp.int32)
    match = target[None, :] == positions[:, None]
    source = jnp.sum(jnp.where(match, slots[None, :], 0), axis=1)
    source = source.reshape(devices_rows, per_slot)

    present = jnp.any(match, axis=1)
    labels = jnp.where(present, jnp.take(block_ids, jnp.sum(jnp.where(match, slots[None, :], 0), axis=1), mode="clip"), -1)
    labels = labels.reshape(devices_rows, per_slot).astype(jnp.float32)

    early = per_slot // 8
    middle = per_slot // 2
    bounds = [(0, early), (early, early + middle), (early + middle, per_slot)]

    def prepare(lo, hi, with_labels):
        if hi <= lo:
            return None
        chunk_source = source[:, lo:hi].reshape(-1)
        outgoing = jnp.take(blocks, chunk_source, axis=0, mode="clip")
        if with_labels:
            tile = jnp.zeros((devices_rows, 8, width), jnp.float32)
            tile = tile.at[:, 0, :per_slot].set(labels)
            outgoing = outgoing.reshape(devices_rows, (hi - lo) * block_rows, width)
            outgoing = jnp.concatenate([outgoing, tile], axis=1)
        return outgoing

    def send(lo, hi, outgoing, after, with_labels):
        if outgoing is None:
            return None, None
        if after is not None:
            outgoing = _gate(outgoing, [after])
        arrived = lax.all_to_all(outgoing, "rows", split_axis=0, concat_axis=0, tiled=True)
        if not with_labels:
            return arrived, None
        got = arrived[:, (hi - lo) * block_rows, :per_slot].astype(jnp.int32)
        data = arrived[:, : (hi - lo) * block_rows].reshape(-1, block_rows, width)
        return data, got

    def masked_gram(rows_of):
        kept = jnp.where(valid[:, None, None], rows_of.reshape(capacity, block_rows, width), 0.0)
        return (
            lax.dot_general(
                kept.reshape(-1, width),
                rows_of,
                (((0,), (0,)), ((), ())),
                precision=lax.Precision.HIGHEST,
                preferred_element_type=jnp.float32,
            )
            / total
        )

    arrived = [None, None, None]
    carrier = [k for k, (lo, hi) in enumerate(bounds) if hi > lo][0]
    outgoing = [prepare(lo, hi, carrier == k) for k, (lo, hi) in enumerate(bounds)]
    flat = blocks.reshape(-1, width)
    arrived[0], got0 = send(*bounds[0], outgoing[0], None, carrier == 0)
    gram_one = _gate(masked_gram(flat), [arrived[0], outgoing[1], outgoing[2]])
    reduced_one = reduce_gram(gram_one)
    arrived[1], got1 = send(*bounds[1], outgoing[1], reduced_one, carrier == 1)
    lower_one, inverse_one = factor(reduced_one)
    first_held = apply_inverse(flat, inverse_one)
    gram_two = _gate(masked_gram(first_held), [arrived[1]])
    reduced_two = reduce_gram(gram_two)
    arrived[2], got2 = send(*bounds[2], outgoing[2], reduced_two, carrier == 2)
    lower_two, inverse_two = factor(reduced_two)
    arrived_labels = [got0, got1, got2][carrier]

    pieces = []
    piece_labels = []
    for (lo, hi), chunk in zip(bounds, arrived):
        if chunk is None:
            continue
        pieces.append(chunk)
        piece_labels.append(arrived_labels[:, lo:hi].reshape(-1))
    all_arrived = jnp.concatenate(pieces, axis=0)
    all_labels = jnp.concatenate(piece_labels, axis=0)
    wanted = own_index * BLK_DEV + jnp.arange(BLK_DEV, dtype=jnp.int32)
    hit = all_labels[None, :] == wanted[:, None]
    place = jnp.sum(jnp.where(hit, positions[None, :], 0), axis=1)
    resident = jnp.take(all_arrived, place, axis=0, mode="clip").reshape(-1, width)
    first = apply_inverse(resident, inverse_one)
    second = apply_inverse(first, inverse_two)
    result = second.reshape(BLK_DEV, block_rows, width)
    r_factor = jnp.dot(
        lower_two.T,
        lower_one.T,
        precision=lax.Precision.HIGHEST,
        preferred_element_type=jnp.float32,
    )
    return (result[:, None], r_factor)


def solution(mesh):
    in_specs = (P("rows", "sub", None, None), P("rows", "sub"), P("rows", "sub"))
    out_specs = (P("rows", "sub", None, None), P())
    return jax.shard_map(
        per_device, mesh=mesh, in_specs=in_specs, out_specs=out_specs, check_vma=False
    )
```

```python
import jax
import jax.numpy as jnp
from jax import lax
from jax.sharding import PartitionSpec as P

BLK_DEV = 32


def _mm(a, b):
    return jnp.dot(a, b, precision=lax.Precision.HIGHEST, preferred_element_type=jnp.float32)


def _lower_inverse(lower):
    identity = jnp.eye(lower.shape[0], dtype=lower.dtype)
    return lax.linalg.triangular_solve(lower, identity, left_side=True, lower=True)


def factor(gram):
    n = gram.shape[0]
    if n % 2 or n < 256:
        lower = jnp.linalg.cholesky(gram)
        return (lower, _lower_inverse(lower))
    k = n // 2
    lower_11 = jnp.linalg.cholesky(gram[:k, :k])
    inverse_11 = _lower_inverse(lower_11)
    lower_21 = _mm(gram[k:, :k], inverse_11.T)
    lower_22 = jnp.linalg.cholesky(gram[k:, k:] - _mm(lower_21, lower_21.T))
    inverse_22 = _lower_inverse(lower_22)
    inverse_21 = -_mm(inverse_22, _mm(lower_21, inverse_11))
    zeros = jnp.zeros((k, n - k), gram.dtype)
    lower = jnp.block([[lower_11, zeros], [lower_21, lower_22]])
    inverse = jnp.block([[inverse_11, zeros], [inverse_21, inverse_22]])
    return (lower, inverse)


def gram_of(flattened, total):
    return (
        lax.dot_general(
            flattened,
            flattened,
            (((0,), (0,)), ((), ())),
            precision=lax.Precision.HIGHEST,
            preferred_element_type=jnp.float32,
        )
        / total
    )


def apply_inverse(flattened, inverse):
    return jnp.dot(
        flattened, inverse.T, precision=lax.Precision.HIGHEST, preferred_element_type=jnp.float32
    )


def _xor_pairs(n, bit):
    return [(i, i ^ bit) for i in range(n)]


def _power_of_two(n):
    return n > 0 and (n & (n - 1)) == 0


def reduce_gram(partial_value):
    n_sub = lax.axis_size("sub")
    n_rows = lax.axis_size("rows")
    width = partial_value.shape[0]
    if not (_power_of_two(n_sub) and _power_of_two(n_rows) and n_sub >= 2 and width % 2 == 0):
        return lax.psum(partial_value, ("rows", "sub"))
    x = partial_value + lax.ppermute(partial_value, "sub", _xor_pairs(n_sub, 1))
    half = width // 2
    h = lax.axis_index("sub") % 2
    y = lax.dynamic_slice_in_dim(x, h * half, half, 0)
    bit = 2
    while bit < n_sub:
        y = y + lax.ppermute(y, "sub", _xor_pairs(n_sub, bit))
        bit *= 2
    bit = 1
    while bit < n_rows:
        y = y + lax.ppermute(y, "rows", _xor_pairs(n_rows, bit))
        bit *= 2
    other = lax.ppermute(y, "sub", _xor_pairs(n_sub, 1))
    first_half = jnp.where(h == 0, y, other)
    second_half = jnp.where(h == 0, other, y)
    return jnp.concatenate([first_half, second_half], axis=0)


def _gate(value, deps):
    flag = jnp.zeros((), jnp.bool_)
    for dep in deps:
        if dep is None:
            continue
        probe = dep[(0,) * dep.ndim]
        flag = flag | (probe != probe)
    corner = value[(slice(0, 1),) * value.ndim]
    kept = jnp.where(flag, jnp.zeros_like(corner), corner)
    return lax.dynamic_update_slice(value, kept, (0,) * value.ndim)


def per_device(held, held_block, held_count):
    capacity = held.shape[0]
    block_rows = held.shape[2]
    width = held.shape[3]
    devices_rows = lax.axis_size("rows")
    own_index = lax.axis_index("rows")
    per_slot = max(1, capacity // devices_rows)
    n_out = devices_rows * per_slot
    total = float(devices_rows * lax.axis_size("sub") * BLK_DEV * block_rows)
    blocks = held[:, 0]
    block_ids = held_block[:, 0]
    count = held_count[0, 0]
    slots = jnp.arange(capacity, dtype=jnp.int32)
    valid = slots < count

    def route(ids, filled):
        destination = ids // BLK_DEV
        earlier = (
            (destination[:, None] == destination[None, :])
            & filled[None, :]
            & (slots[None, :] < slots[:, None])
        )
        rank_within = jnp.sum(earlier.astype(jnp.int32), axis=1)
        return jnp.where(filled, destination * per_slot + rank_within, n_out)

    target = route(block_ids, valid)
    positions = jnp.arange(n_out, dtype=jnp.int32)
    match = target[None, :] == positions[:, None]
    source = jnp.sum(jnp.where(match, slots[None, :], 0), axis=1)
    source = source.reshape(devices_rows, per_slot)

    present = jnp.any(match, axis=1)
    labels = jnp.where(present, jnp.take(block_ids, jnp.sum(jnp.where(match, slots[None, :], 0), axis=1), mode="clip"), -1)
    labels = labels.reshape(devices_rows, per_slot).astype(jnp.float32)

    early = per_slot // 4
    middle = (per_slot - early) // 2
    bounds = [(0, early), (early, early + middle), (early + middle, per_slot)]

    def prepare(lo, hi, with_labels):
        if hi <= lo:
            return None
        chunk_source = source[:, lo:hi].reshape(-1)
        outgoing = jnp.take(blocks, chunk_source, axis=0, mode="clip")
        if with_labels:
            tile = jnp.zeros((devices_rows, 8, width), jnp.float32)
            tile = tile.at[:, 0, :per_slot].set(labels)
            outgoing = outgoing.reshape(devices_rows, (hi - lo) * block_rows, width)
            outgoing = jnp.concatenate([outgoing, tile], axis=1)
        return outgoing

    def send(lo, hi, outgoing, after, with_labels):
        if outgoing is None:
            return None, None
        if after is not None:
            outgoing = _gate(outgoing, [after])
        arrived = lax.all_to_all(outgoing, "rows", split_axis=0, concat_axis=0, tiled=True)
        if not with_labels:
            return arrived, None
        got = arrived[:, (hi - lo) * block_rows, :per_slot].astype(jnp.int32)
        data = arrived[:, : (hi - lo) * block_rows].reshape(-1, block_rows, width)
        return data, got

    def masked_gram(rows_of):
        kept = jnp.where(valid[:, None, None], rows_of.reshape(capacity, block_rows, width), 0.0)
        return (
            lax.dot_general(
                kept.reshape(-1, width),
                rows_of,
                (((0,), (0,)), ((), ())),
                precision=lax.Precision.HIGHEST,
                preferred_element_type=jnp.float32,
            )
            / total
        )

    arrived = [None, None, None]
    carrier = [k for k, (lo, hi) in enumerate(bounds) if hi > lo][0]
    outgoing = [prepare(lo, hi, carrier == k) for k, (lo, hi) in enumerate(bounds)]
    flat = blocks.reshape(-1, width)
    arrived[0], got0 = send(*bounds[0], outgoing[0], None, carrier == 0)
    gram_one = _gate(masked_gram(flat), [arrived[0], outgoing[1], outgoing[2]])
    reduced_one = reduce_gram(gram_one)
    arrived[1], got1 = send(*bounds[1], outgoing[1], reduced_one, carrier == 1)
    lower_one, inverse_one = factor(reduced_one)
    first_held = apply_inverse(flat, inverse_one)
    gram_two = _gate(masked_gram(first_held), [arrived[1]])
    reduced_two = reduce_gram(gram_two)
    arrived[2], got2 = send(*bounds[2], outgoing[2], reduced_two, carrier == 2)
    lower_two, inverse_two = factor(reduced_two)
    arrived_labels = [got0, got1, got2][carrier]

    pieces = []
    piece_labels = []
    for (lo, hi), chunk in zip(bounds, arrived):
        if chunk is None:
            continue
        pieces.append(chunk)
        piece_labels.append(arrived_labels[:, lo:hi].reshape(-1))
    all_arrived = jnp.concatenate(pieces, axis=0)
    all_labels = jnp.concatenate(piece_labels, axis=0)
    wanted = own_index * BLK_DEV + jnp.arange(BLK_DEV, dtype=jnp.int32)
    hit = all_labels[None, :] == wanted[:, None]
    place = jnp.sum(jnp.where(hit, positions[None, :], 0), axis=1)
    resident = jnp.take(all_arrived, place, axis=0, mode="clip").reshape(-1, width)
    first = apply_inverse(resident, inverse_one)
    second = apply_inverse(first, inverse_two)
    result = second.reshape(BLK_DEV, block_rows, width)
    r_factor = jnp.dot(
        lower_two.T,
        lower_one.T,
        precision=lax.Precision.HIGHEST,
        preferred_element_type=jnp.float32,
    )
    return (result[:, None], r_factor)


def solution(mesh):
    in_specs = (P("rows", "sub", None, None), P("rows", "sub"), P("rows", "sub"))
    out_specs = (P("rows", "sub", None, None), P())
    return jax.shard_map(
        per_device, mesh=mesh, in_specs=in_specs, out_specs=out_specs, check_vma=False
    )
```

```python
import jax
import jax.numpy as jnp
from jax import lax
from jax.sharding import PartitionSpec as P

BLK_DEV = 32


def _mm(a, b):
    return jnp.dot(a, b, precision=lax.Precision.HIGHEST, preferred_element_type=jnp.float32)


def _lower_inverse(lower):
    identity = jnp.eye(lower.shape[0], dtype=lower.dtype)
    return lax.linalg.triangular_solve(lower, identity, left_side=True, lower=True)


def factor(gram):
    n = gram.shape[0]
    if n % 2 or n < 256:
        lower = jnp.linalg.cholesky(gram)
        return (lower, _lower_inverse(lower))
    k = n // 2
    lower_11 = jnp.linalg.cholesky(gram[:k, :k])
    inverse_11 = _lower_inverse(lower_11)
    lower_21 = _mm(gram[k:, :k], inverse_11.T)
    lower_22 = jnp.linalg.cholesky(gram[k:, k:] - _mm(lower_21, lower_21.T))
    inverse_22 = _lower_inverse(lower_22)
    inverse_21 = -_mm(inverse_22, _mm(lower_21, inverse_11))
    zeros = jnp.zeros((k, n - k), gram.dtype)
    lower = jnp.block([[lower_11, zeros], [lower_21, lower_22]])
    inverse = jnp.block([[inverse_11, zeros], [inverse_21, inverse_22]])
    return (lower, inverse)


def gram_of(flattened, total):
    return (
        lax.dot_general(
            flattened,
            flattened,
            (((0,), (0,)), ((), ())),
            precision=lax.Precision.HIGHEST,
            preferred_element_type=jnp.float32,
        )
        / total
    )


def apply_inverse(flattened, inverse):
    return jnp.dot(
        flattened, inverse.T, precision=lax.Precision.HIGHEST, preferred_element_type=jnp.float32
    )


def _xor_pairs(n, bit):
    return [(i, i ^ bit) for i in range(n)]


def _power_of_two(n):
    return n > 0 and (n & (n - 1)) == 0


def reduce_gram(partial_value):
    n_sub = lax.axis_size("sub")
    n_rows = lax.axis_size("rows")
    width = partial_value.shape[0]
    if not (_power_of_two(n_sub) and _power_of_two(n_rows) and n_sub >= 2 and width % 2 == 0):
        return lax.psum(partial_value, ("rows", "sub"))
    x = partial_value + lax.ppermute(partial_value, "sub", _xor_pairs(n_sub, 1))
    half = width // 2
    h = lax.axis_index("sub") % 2
    y = lax.dynamic_slice_in_dim(x, h * half, half, 0)
    bit = 2
    while bit < n_sub:
        y = y + lax.ppermute(y, "sub", _xor_pairs(n_sub, bit))
        bit *= 2
    bit = 1
    while bit < n_rows:
        y = y + lax.ppermute(y, "rows", _xor_pairs(n_rows, bit))
        bit *= 2
    other = lax.ppermute(y, "sub", _xor_pairs(n_sub, 1))
    first_half = jnp.where(h == 0, y, other)
    second_half = jnp.where(h == 0, other, y)
    return jnp.concatenate([first_half, second_half], axis=0)


def _gate(value, deps):
    flag = jnp.zeros((), jnp.bool_)
    for dep in deps:
        if dep is None:
            continue
        probe = dep[(0,) * dep.ndim]
        flag = flag | (probe != probe)
    corner = value[(slice(0, 1),) * value.ndim]
    kept = jnp.where(flag, jnp.zeros_like(corner), corner)
    return lax.dynamic_update_slice(value, kept, (0,) * value.ndim)


def per_device(held, held_block, held_count):
    capacity = held.shape[0]
    block_rows = held.shape[2]
    width = held.shape[3]
    devices_rows = lax.axis_size("rows")
    own_index = lax.axis_index("rows")
    per_slot = max(1, capacity // devices_rows)
    n_out = devices_rows * per_slot
    total = float(devices_rows * lax.axis_size("sub") * BLK_DEV * block_rows)
    blocks = held[:, 0]
    block_ids = held_block[:, 0]
    count = held_count[0, 0]
    slots = jnp.arange(capacity, dtype=jnp.int32)
    valid = slots < count

    def route(ids, filled):
        destination = ids // BLK_DEV
        earlier = (
            (destination[:, None] == destination[None, :])
            & filled[None, :]
            & (slots[None, :] < slots[:, None])
        )
        rank_within = jnp.sum(earlier.astype(jnp.int32), axis=1)
        return jnp.where(filled, destination * per_slot + rank_within, n_out)

    target = route(block_ids, valid)
    positions = jnp.arange(n_out, dtype=jnp.int32)
    match = target[None, :] == positions[:, None]
    source = jnp.sum(jnp.where(match, slots[None, :], 0), axis=1)
    source = source.reshape(devices_rows, per_slot)

    present = jnp.any(match, axis=1)
    labels = jnp.where(present, jnp.take(block_ids, jnp.sum(jnp.where(match, slots[None, :], 0), axis=1), mode="clip"), -1)
    labels = labels.reshape(devices_rows, per_slot).astype(jnp.float32)

    early = per_slot // 4
    middle = (per_slot - early) // 2
    bounds = [(0, early), (early, early + middle), (early + middle, per_slot)]

    def prepare(lo, hi, with_labels):
        if hi <= lo:
            return None
        chunk_source = source[:, lo:hi].reshape(-1)
        outgoing = jnp.take(blocks, chunk_source, axis=0, mode="clip")
        if with_labels:
            tile = jnp.zeros((devices_rows, 8, width), jnp.float32)
            tile = tile.at[:, 0, :per_slot].set(labels)
            outgoing = outgoing.reshape(devices_rows, (hi - lo) * block_rows, width)
            outgoing = jnp.concatenate([outgoing, tile], axis=1)
        return outgoing

    def send(lo, hi, outgoing, after, with_labels):
        if outgoing is None:
            return None, None
        if after is not None:
            outgoing = _gate(outgoing, [after])
        arrived = lax.all_to_all(outgoing, "rows", split_axis=0, concat_axis=0, tiled=True)
        if not with_labels:
            return arrived, None
        got = arrived[:, (hi - lo) * block_rows, :per_slot].astype(jnp.int32)
        data = arrived[:, : (hi - lo) * block_rows].reshape(-1, block_rows, width)
        return data, got

    def masked_gram(rows_of):
        kept = jnp.where(valid[:, None, None], rows_of.reshape(capacity, block_rows, width), 0.0)
        return (
            lax.dot_general(
                kept.reshape(-1, width),
                rows_of,
                (((0,), (0,)), ((), ())),
                precision=lax.Precision.HIGHEST,
                preferred_element_type=jnp.float32,
            )
            / total
        )

    arrived = [None, None, None]
    carrier = [k for k, (lo, hi) in enumerate(bounds) if hi > lo][0]
    outgoing = [prepare(lo, hi, carrier == k) for k, (lo, hi) in enumerate(bounds)]
    flat = blocks.reshape(-1, width)
    arrived[0], got0 = send(*bounds[0], outgoing[0], None, carrier == 0)
    gram_one = _gate(masked_gram(flat), [arrived[0], outgoing[1], outgoing[2]])
    reduced_one = reduce_gram(gram_one)
    arrived[1], got1 = send(*bounds[1], outgoing[1], reduced_one, carrier == 1)
    lower_one, inverse_one = factor(reduced_one)
    first_held = apply_inverse(flat, inverse_one)
    gram_two = _gate(masked_gram(first_held), [arrived[1]])
    reduced_two = reduce_gram(gram_two)
    arrived[2], got2 = send(*bounds[2], outgoing[2], reduced_two, carrier == 2)
    lower_two, inverse_two = factor(reduced_two)
    arrived_labels = [got0, got1, got2][carrier]

    wanted = own_index * BLK_DEV + jnp.arange(BLK_DEV, dtype=jnp.int32)
    combined = _mm(inverse_one.T, inverse_two.T)
    resident = None
    for (lo, hi), chunk in zip(bounds, arrived):
        if chunk is None:
            continue
        chunk_labels = arrived_labels[:, lo:hi].reshape(-1)
        pick = (chunk_labels[None, :] == wanted[:, None]).astype(jnp.float32)
        picked = lax.dot_general(
            pick,
            chunk,
            (((1,), (0,)), ((), ())),
            precision=lax.Precision.HIGHEST,
            preferred_element_type=jnp.float32,
        )
        resident = picked if resident is None else resident + picked
    resident = resident.reshape(-1, width)
    second = apply_inverse(resident, combined.T)
    result = second.reshape(BLK_DEV, block_rows, width)
    r_factor = jnp.dot(
        lower_two.T,
        lower_one.T,
        precision=lax.Precision.HIGHEST,
        preferred_element_type=jnp.float32,
    )
    return (result[:, None], r_factor)


def solution(mesh):
    in_specs = (P("rows", "sub", None, None), P("rows", "sub"), P("rows", "sub"))
    out_specs = (P("rows", "sub", None, None), P())
    return jax.shard_map(
        per_device, mesh=mesh, in_specs=in_specs, out_specs=out_specs, check_vma=False
    )
```

```python
import jax
import jax.numpy as jnp
from jax import lax
from jax.sharding import PartitionSpec as P

BLK_DEV = 32


def _mm(a, b):
    return jnp.dot(a, b, precision=lax.Precision.HIGHEST, preferred_element_type=jnp.float32)


def _lower_inverse(lower):
    identity = jnp.eye(lower.shape[0], dtype=lower.dtype)
    return lax.linalg.triangular_solve(lower, identity, left_side=True, lower=True)


def factor(gram):
    n = gram.shape[0]
    if n % 2 or n < 256:
        lower = jnp.linalg.cholesky(gram)
        return (lower, _lower_inverse(lower))
    k = n // 2
    lower_11 = jnp.linalg.cholesky(gram[:k, :k])
    inverse_11 = _lower_inverse(lower_11)
    lower_21 = _mm(gram[k:, :k], inverse_11.T)
    lower_22 = jnp.linalg.cholesky(gram[k:, k:] - _mm(lower_21, lower_21.T))
    inverse_22 = _lower_inverse(lower_22)
    inverse_21 = -_mm(inverse_22, _mm(lower_21, inverse_11))
    zeros = jnp.zeros((k, n - k), gram.dtype)
    lower = jnp.block([[lower_11, zeros], [lower_21, lower_22]])
    inverse = jnp.block([[inverse_11, zeros], [inverse_21, inverse_22]])
    return (lower, inverse)


def gram_of(flattened, total):
    return (
        lax.dot_general(
            flattened,
            flattened,
            (((0,), (0,)), ((), ())),
            precision=lax.Precision.HIGHEST,
            preferred_element_type=jnp.float32,
        )
        / total
    )


def apply_inverse(flattened, inverse):
    return jnp.dot(
        flattened, inverse.T, precision=lax.Precision.HIGHEST, preferred_element_type=jnp.float32
    )


def _xor_pairs(n, bit):
    return [(i, i ^ bit) for i in range(n)]


def _power_of_two(n):
    return n > 0 and (n & (n - 1)) == 0


def reduce_gram(partial_value, hold=None):
    n_sub = lax.axis_size("sub")
    n_rows = lax.axis_size("rows")
    width = partial_value.shape[0]
    if not (_power_of_two(n_sub) and _power_of_two(n_rows) and n_sub >= 2 and width % 2 == 0):
        total = lax.psum(_gate(partial_value, hold or []), ("rows", "sub"))
        return total, total
    half = width // 2
    h = lax.axis_index("sub") % 2
    mine = lax.dynamic_slice_in_dim(partial_value, h * half, half, 0)
    theirs = lax.dynamic_slice_in_dim(partial_value, (1 - h) * half, half, 0)
    y = mine + lax.ppermute(theirs, "sub", _xor_pairs(n_sub, 1))
    bit = 2
    while bit < n_sub:
        y = y + lax.ppermute(y, "sub", _xor_pairs(n_sub, bit))
        bit *= 2
    if hold:
        y = _gate(y, hold)
    bit = 1
    while bit < n_rows:
        y = y + lax.ppermute(y, "rows", _xor_pairs(n_rows, bit))
        bit *= 2
    other = lax.ppermute(y, "sub", _xor_pairs(n_sub, 1))
    first_half = jnp.where(h == 0, y, other)
    second_half = jnp.where(h == 0, other, y)
    return jnp.concatenate([first_half, second_half], axis=0), y


def _gate(value, deps):
    flag = jnp.zeros((), jnp.bool_)
    for dep in deps:
        if dep is None:
            continue
        probe = dep[(0,) * dep.ndim]
        flag = flag | (probe != probe)
    corner = value[(slice(0, 1),) * value.ndim]
    kept = jnp.where(flag, jnp.zeros_like(corner), corner)
    return lax.dynamic_update_slice(value, kept, (0,) * value.ndim)


def per_device(held, held_block, held_count):
    capacity = held.shape[0]
    block_rows = held.shape[2]
    width = held.shape[3]
    devices_rows = lax.axis_size("rows")
    own_index = lax.axis_index("rows")
    per_slot = max(1, capacity // devices_rows)
    n_out = devices_rows * per_slot
    total = float(devices_rows * lax.axis_size("sub") * BLK_DEV * block_rows)
    blocks = held[:, 0]
    block_ids = held_block[:, 0]
    count = held_count[0, 0]
    slots = jnp.arange(capacity, dtype=jnp.int32)
    valid = slots < count

    def route(ids, filled):
        destination = ids // BLK_DEV
        earlier = (
            (destination[:, None] == destination[None, :])
            & filled[None, :]
            & (slots[None, :] < slots[:, None])
        )
        rank_within = jnp.sum(earlier.astype(jnp.int32), axis=1)
        return jnp.where(filled, destination * per_slot + rank_within, n_out)

    target = route(block_ids, valid)
    positions = jnp.arange(n_out, dtype=jnp.int32)
    match = target[None, :] == positions[:, None]
    source = jnp.sum(jnp.where(match, slots[None, :], 0), axis=1)
    source = source.reshape(devices_rows, per_slot)

    present = jnp.any(match, axis=1)
    labels = jnp.where(present, jnp.take(block_ids, jnp.sum(jnp.where(match, slots[None, :], 0), axis=1), mode="clip"), -1)
    labels = labels.reshape(devices_rows, per_slot).astype(jnp.float32)

    early = per_slot // 4
    middle = (per_slot - early) // 2
    bounds = [(0, early), (early, early + middle), (early + middle, per_slot)]

    def prepare(lo, hi, with_labels):
        if hi <= lo:
            return None
        chunk_source = source[:, lo:hi].reshape(-1)
        outgoing = jnp.take(blocks, chunk_source, axis=0, mode="clip")
        if with_labels:
            tile = jnp.zeros((devices_rows, 8, width), jnp.float32)
            tile = tile.at[:, 0, :per_slot].set(labels)
            outgoing = outgoing.reshape(devices_rows, (hi - lo) * block_rows, width)
            outgoing = jnp.concatenate([outgoing, tile], axis=1)
        return outgoing

    def send(lo, hi, outgoing, after, with_labels):
        if outgoing is None:
            return None, None
        if after is not None:
            outgoing = _gate(outgoing, [after])
        arrived = lax.all_to_all(outgoing, "rows", split_axis=0, concat_axis=0, tiled=True)
        if not with_labels:
            return arrived, None
        got = arrived[:, (hi - lo) * block_rows, :per_slot].astype(jnp.int32)
        data = arrived[:, : (hi - lo) * block_rows].reshape(-1, block_rows, width)
        return data, got

    def masked_gram(rows_of):
        kept = jnp.where(valid[:, None, None], rows_of.reshape(capacity, block_rows, width), 0.0)
        return (
            lax.dot_general(
                kept.reshape(-1, width),
                rows_of,
                (((0,), (0,)), ((), ())),
                precision=lax.Precision.HIGHEST,
                preferred_element_type=jnp.float32,
            )
            / total
        )

    arrived = [None, None, None]
    carrier = [k for k, (lo, hi) in enumerate(bounds) if hi > lo][0]
    outgoing = [prepare(lo, hi, carrier == k) for k, (lo, hi) in enumerate(bounds)]
    flat = blocks.reshape(-1, width)
    arrived[0], got0 = send(*bounds[0], outgoing[0], None, carrier == 0)
    gram_one = _gate(masked_gram(flat), [outgoing[1], outgoing[2]])
    reduced_one, rows_one = reduce_gram(gram_one, [arrived[0]])
    arrived[1], got1 = send(*bounds[1], outgoing[1], rows_one, carrier == 1)
    lower_one, inverse_one = factor(reduced_one)
    first_held = apply_inverse(flat, inverse_one)
    reduced_two, rows_two = reduce_gram(masked_gram(first_held), [arrived[1]])
    arrived[2], got2 = send(*bounds[2], outgoing[2], rows_two, carrier == 2)
    lower_two, inverse_two = factor(reduced_two)
    arrived_labels = [got0, got1, got2][carrier]

    wanted = own_index * BLK_DEV + jnp.arange(BLK_DEV, dtype=jnp.int32)
    combined = _mm(inverse_one.T, inverse_two.T)
    resident = None
    for (lo, hi), chunk in zip(bounds, arrived):
        if chunk is None:
            continue
        chunk_labels = arrived_labels[:, lo:hi].reshape(-1)
        pick = (chunk_labels[None, :] == wanted[:, None]).astype(jnp.float32)
        picked = lax.dot_general(
            pick,
            chunk,
            (((1,), (0,)), ((), ())),
            precision=lax.Precision.HIGHEST,
            preferred_element_type=jnp.float32,
        )
        resident = picked if resident is None else resident + picked
    resident = resident.reshape(-1, width)
    second = apply_inverse(resident, combined.T)
    result = second.reshape(BLK_DEV, block_rows, width)
    r_factor = jnp.dot(
        lower_two.T,
        lower_one.T,
        precision=lax.Precision.HIGHEST,
        preferred_element_type=jnp.float32,
    )
    return (result[:, None], r_factor)


def solution(mesh):
    in_specs = (P("rows", "sub", None, None), P("rows", "sub"), P("rows", "sub"))
    out_specs = (P("rows", "sub", None, None), P())
    return jax.shard_map(
        per_device, mesh=mesh, in_specs=in_specs, out_specs=out_specs, check_vma=False
    )
```

```python
import jax
import jax.numpy as jnp
from jax import lax
from jax.sharding import PartitionSpec as P

BLK_DEV = 32


def _mm(a, b):
    return jnp.dot(a, b, precision=lax.Precision.HIGHEST, preferred_element_type=jnp.float32)


def _lower_inverse(lower):
    identity = jnp.eye(lower.shape[0], dtype=lower.dtype)
    return lax.linalg.triangular_solve(lower, identity, left_side=True, lower=True)


def factor(gram):
    n = gram.shape[0]
    if n % 2 or n < 256:
        lower = jnp.linalg.cholesky(gram)
        return (lower, _lower_inverse(lower))
    k = n // 2
    lower_11 = jnp.linalg.cholesky(gram[:k, :k])
    inverse_11 = _lower_inverse(lower_11)
    lower_21 = _mm(gram[k:, :k], inverse_11.T)
    lower_22 = jnp.linalg.cholesky(gram[k:, k:] - _mm(lower_21, lower_21.T))
    inverse_22 = _lower_inverse(lower_22)
    inverse_21 = -_mm(inverse_22, _mm(lower_21, inverse_11))
    zeros = jnp.zeros((k, n - k), gram.dtype)
    lower = jnp.block([[lower_11, zeros], [lower_21, lower_22]])
    inverse = jnp.block([[inverse_11, zeros], [inverse_21, inverse_22]])
    return (lower, inverse)


def gram_of(flattened, total):
    return (
        lax.dot_general(
            flattened,
            flattened,
            (((0,), (0,)), ((), ())),
            precision=lax.Precision.HIGHEST,
            preferred_element_type=jnp.float32,
        )
        / total
    )


def apply_inverse(flattened, inverse):
    return jnp.dot(
        flattened, inverse.T, precision=lax.Precision.HIGHEST, preferred_element_type=jnp.float32
    )


def _xor_pairs(n, bit):
    return [(i, i ^ bit) for i in range(n)]


def _power_of_two(n):
    return n > 0 and (n & (n - 1)) == 0


def reduce_gram(partial_value, hold=None):
    n_sub = lax.axis_size("sub")
    n_rows = lax.axis_size("rows")
    width = partial_value.shape[0]
    if not (_power_of_two(n_sub) and _power_of_two(n_rows) and n_sub >= 2 and width % 2 == 0):
        total = lax.psum(_gate(partial_value, hold or []), ("rows", "sub"))
        return total, total
    k = width // 2
    h = lax.axis_index("sub") % 2
    row = lax.broadcasted_iota(jnp.int32, (k, k), 0)
    col = lax.broadcasted_iota(jnp.int32, (k, k), 1)
    folded = jnp.where(row >= col, partial_value[:k, :k], partial_value[k:, k:].T)
    spare = jnp.zeros((8, k), partial_value.dtype)
    pack_0 = jnp.concatenate([partial_value[k:, :k], spare], axis=0)
    spare_1 = spare.at[0].set(jnp.diagonal(partial_value[k:, k:]))
    pack_1 = jnp.concatenate([folded, spare_1], axis=0)
    mine = jnp.where(h == 0, pack_0, pack_1)
    theirs = jnp.where(h == 0, pack_1, pack_0)
    y = mine + lax.ppermute(theirs, "sub", _xor_pairs(n_sub, 1))
    bit = 2
    while bit < n_sub:
        y = y + lax.ppermute(y, "sub", _xor_pairs(n_sub, bit))
        bit *= 2
    if hold:
        y = _gate(y, hold)
    bit = 1
    while bit < n_rows:
        y = y + lax.ppermute(y, "rows", _xor_pairs(n_rows, bit))
        bit *= 2
    other = lax.ppermute(y, "sub", _xor_pairs(n_sub, 1))
    off = jnp.where(h == 0, y, other)[:k]
    both = jnp.where(h == 0, other, y)
    tri = both[:k]
    upper_left = jnp.where(row >= col, tri, tri.T)
    lower_right = jnp.where(row > col, tri.T, jnp.where(row < col, tri, both[k][None, :]))
    full = jnp.concatenate(
        [jnp.concatenate([upper_left, off.T], axis=1), jnp.concatenate([off, lower_right], axis=1)],
        axis=0,
    )
    return full, y


def _gate(value, deps):
    flag = jnp.zeros((), jnp.bool_)
    for dep in deps:
        if dep is None:
            continue
        probe = dep[(0,) * dep.ndim]
        flag = flag | (probe != probe)
    corner = value[(slice(0, 1),) * value.ndim]
    kept = jnp.where(flag, jnp.zeros_like(corner), corner)
    return lax.dynamic_update_slice(value, kept, (0,) * value.ndim)


def per_device(held, held_block, held_count):
    capacity = held.shape[0]
    block_rows = held.shape[2]
    width = held.shape[3]
    devices_rows = lax.axis_size("rows")
    own_index = lax.axis_index("rows")
    per_slot = max(1, capacity // devices_rows)
    n_out = devices_rows * per_slot
    total = float(devices_rows * lax.axis_size("sub") * BLK_DEV * block_rows)
    blocks = held[:, 0]
    block_ids = held_block[:, 0]
    count = held_count[0, 0]
    slots = jnp.arange(capacity, dtype=jnp.int32)
    valid = slots < count

    def route(ids, filled):
        destination = ids // BLK_DEV
        earlier = (
            (destination[:, None] == destination[None, :])
            & filled[None, :]
            & (slots[None, :] < slots[:, None])
        )
        rank_within = jnp.sum(earlier.astype(jnp.int32), axis=1)
        return jnp.where(filled, destination * per_slot + rank_within, n_out)

    target = route(block_ids, valid)
    positions = jnp.arange(n_out, dtype=jnp.int32)
    match = target[None, :] == positions[:, None]
    source = jnp.sum(jnp.where(match, slots[None, :], 0), axis=1)
    source = source.reshape(devices_rows, per_slot)

    present = jnp.any(match, axis=1)
    labels = jnp.where(present, jnp.take(block_ids, jnp.sum(jnp.where(match, slots[None, :], 0), axis=1), mode="clip"), -1)
    labels = labels.reshape(devices_rows, per_slot).astype(jnp.float32)

    early = per_slot // 4
    middle = (per_slot - early) // 2
    bounds = [(0, early), (early, early + middle), (early + middle, per_slot)]

    def prepare(lo, hi, with_labels):
        if hi <= lo:
            return None
        chunk_source = source[:, lo:hi].reshape(-1)
        outgoing = jnp.take(blocks, chunk_source, axis=0, mode="clip")
        if with_labels:
            tile = jnp.zeros((devices_rows, 8, width), jnp.float32)
            tile = tile.at[:, 0, :per_slot].set(labels)
            outgoing = outgoing.reshape(devices_rows, (hi - lo) * block_rows, width)
            outgoing = jnp.concatenate([outgoing, tile], axis=1)
        return outgoing

    def send(lo, hi, outgoing, after, with_labels):
        if outgoing is None:
            return None, None
        if after is not None:
            outgoing = _gate(outgoing, [after])
        arrived = lax.all_to_all(outgoing, "rows", split_axis=0, concat_axis=0, tiled=True)
        if not with_labels:
            return arrived, None
        got = arrived[:, (hi - lo) * block_rows, :per_slot].astype(jnp.int32)
        data = arrived[:, : (hi - lo) * block_rows].reshape(-1, block_rows, width)
        return data, got

    def masked_gram(rows_of):
        kept = jnp.where(valid[:, None, None], rows_of.reshape(capacity, block_rows, width), 0.0)
        return (
            lax.dot_general(
                kept.reshape(-1, width),
                rows_of,
                (((0,), (0,)), ((), ())),
                precision=lax.Precision.HIGHEST,
                preferred_element_type=jnp.float32,
            )
            / total
        )

    arrived = [None, None, None]
    carrier = [k for k, (lo, hi) in enumerate(bounds) if hi > lo][0]
    outgoing = [prepare(lo, hi, carrier == k) for k, (lo, hi) in enumerate(bounds)]
    flat = blocks.reshape(-1, width)
    arrived[0], got0 = send(*bounds[0], outgoing[0], None, carrier == 0)
    gram_one = _gate(masked_gram(flat), [outgoing[1], outgoing[2]])
    reduced_one, rows_one = reduce_gram(gram_one, [arrived[0]])
    arrived[1], got1 = send(*bounds[1], outgoing[1], rows_one, carrier == 1)
    lower_one, inverse_one = factor(reduced_one)
    first_held = apply_inverse(flat, inverse_one)
    reduced_two, rows_two = reduce_gram(masked_gram(first_held), [arrived[1]])
    arrived[2], got2 = send(*bounds[2], outgoing[2], rows_two, carrier == 2)
    lower_two, inverse_two = factor(reduced_two)
    arrived_labels = [got0, got1, got2][carrier]

    wanted = own_index * BLK_DEV + jnp.arange(BLK_DEV, dtype=jnp.int32)
    combined = _mm(inverse_one.T, inverse_two.T)
    resident = None
    for (lo, hi), chunk in zip(bounds, arrived):
        if chunk is None:
            continue
        chunk_labels = arrived_labels[:, lo:hi].reshape(-1)
        pick = (chunk_labels[None, :] == wanted[:, None]).astype(jnp.float32)
        picked = lax.dot_general(
            pick,
            chunk,
            (((1,), (0,)), ((), ())),
            precision=lax.Precision.HIGHEST,
            preferred_element_type=jnp.float32,
        )
        resident = picked if resident is None else resident + picked
    resident = resident.reshape(-1, width)
    second = apply_inverse(resident, combined.T)
    result = second.reshape(BLK_DEV, block_rows, width)
    r_factor = jnp.dot(
        lower_two.T,
        lower_one.T,
        precision=lax.Precision.HIGHEST,
        preferred_element_type=jnp.float32,
    )
    return (result[:, None], r_factor)


def solution(mesh):
    in_specs = (P("rows", "sub", None, None), P("rows", "sub"), P("rows", "sub"))
    out_specs = (P("rows", "sub", None, None), P())
    return jax.shard_map(
        per_device, mesh=mesh, in_specs=in_specs, out_specs=out_specs, check_vma=False
    )
```

```python
import jax
import jax.numpy as jnp
from jax import lax
from jax.sharding import PartitionSpec as P

BLK_DEV = 32


def _mm(a, b):
    return jnp.dot(a, b, precision=lax.Precision.HIGHEST, preferred_element_type=jnp.float32)


def _lower_inverse(lower):
    identity = jnp.eye(lower.shape[0], dtype=lower.dtype)
    return lax.linalg.triangular_solve(lower, identity, left_side=True, lower=True)


def factor(gram):
    n = gram.shape[0]
    if n % 2 or n < 256:
        lower = jnp.linalg.cholesky(gram)
        return (lower, _lower_inverse(lower))
    k = n // 2
    lower_11 = jnp.linalg.cholesky(gram[:k, :k])
    inverse_11 = _lower_inverse(lower_11)
    lower_21 = _mm(gram[k:, :k], inverse_11.T)
    lower_22 = jnp.linalg.cholesky(gram[k:, k:] - _mm(lower_21, lower_21.T))
    inverse_22 = _lower_inverse(lower_22)
    inverse_21 = -_mm(inverse_22, _mm(lower_21, inverse_11))
    zeros = jnp.zeros((k, n - k), gram.dtype)
    lower = jnp.block([[lower_11, zeros], [lower_21, lower_22]])
    inverse = jnp.block([[inverse_11, zeros], [inverse_21, inverse_22]])
    return (lower, inverse)


def gram_of(flattened, total):
    return (
        lax.dot_general(
            flattened,
            flattened,
            (((0,), (0,)), ((), ())),
            precision=lax.Precision.HIGHEST,
            preferred_element_type=jnp.float32,
        )
        / total
    )


def apply_inverse(flattened, inverse):
    return jnp.dot(
        flattened, inverse.T, precision=lax.Precision.HIGHEST, preferred_element_type=jnp.float32
    )


def _xor_pairs(n, bit):
    return [(i, i ^ bit) for i in range(n)]


def _power_of_two(n):
    return n > 0 and (n & (n - 1)) == 0


def reduce_gram(partial_value, hold=None):
    n_sub = lax.axis_size("sub")
    n_rows = lax.axis_size("rows")
    width = partial_value.shape[0]
    if not (_power_of_two(n_sub) and _power_of_two(n_rows) and n_sub >= 2 and width % 2 == 0):
        total = lax.psum(_gate(partial_value, hold or []), ("rows", "sub"))
        return total, total
    half = width // 2
    h = lax.axis_index("sub") % 2
    mine = lax.dynamic_slice_in_dim(partial_value, h * half, half, 0)
    theirs = lax.dynamic_slice_in_dim(partial_value, (1 - h) * half, half, 0)
    y = mine + lax.ppermute(theirs, "sub", _xor_pairs(n_sub, 1))
    bit = 2
    while bit < n_sub:
        y = y + lax.ppermute(y, "sub", _xor_pairs(n_sub, bit))
        bit *= 2
    if hold:
        y = _gate(y, hold)
    bit = 1
    while bit < n_rows:
        y = y + lax.ppermute(y, "rows", _xor_pairs(n_rows, bit))
        bit *= 2
    other = lax.ppermute(y, "sub", _xor_pairs(n_sub, 1))
    first_half = jnp.where(h == 0, y, other)
    second_half = jnp.where(h == 0, other, y)
    return jnp.concatenate([first_half, second_half], axis=0), y


def _gate(value, deps):
    flag = jnp.zeros((), jnp.bool_)
    for dep in deps:
        if dep is None:
            continue
        probe = dep[(0,) * dep.ndim]
        flag = flag | (probe != probe)
    corner = value[(slice(0, 1),) * value.ndim]
    kept = jnp.where(flag, jnp.zeros_like(corner), corner)
    return lax.dynamic_update_slice(value, kept, (0,) * value.ndim)


def per_device(held, held_block, held_count):
    capacity = held.shape[0]
    block_rows = held.shape[2]
    width = held.shape[3]
    devices_rows = lax.axis_size("rows")
    own_index = lax.axis_index("rows")
    per_slot = max(1, capacity // devices_rows)
    n_out = devices_rows * per_slot
    total = float(devices_rows * lax.axis_size("sub") * BLK_DEV * block_rows)
    blocks = held[:, 0]
    block_ids = held_block[:, 0]
    count = held_count[0, 0]
    slots = jnp.arange(capacity, dtype=jnp.int32)
    valid = slots < count

    def route(ids, filled):
        destination = ids // BLK_DEV
        earlier = (
            (destination[:, None] == destination[None, :])
            & filled[None, :]
            & (slots[None, :] < slots[:, None])
        )
        rank_within = jnp.sum(earlier.astype(jnp.int32), axis=1)
        return jnp.where(filled, destination * per_slot + rank_within, n_out)

    target = route(block_ids, valid)
    positions = jnp.arange(n_out, dtype=jnp.int32)
    match = target[None, :] == positions[:, None]
    source = jnp.sum(jnp.where(match, slots[None, :], 0), axis=1)
    source = source.reshape(devices_rows, per_slot)

    present = jnp.any(match, axis=1)
    labels = jnp.where(present, jnp.take(block_ids, jnp.sum(jnp.where(match, slots[None, :], 0), axis=1), mode="clip"), -1)
    labels = labels.reshape(devices_rows, per_slot).astype(jnp.float32)

    early = per_slot // 4
    middle = (per_slot - early) // 2
    bounds = [(0, early), (early, early + middle), (early + middle, per_slot)]

    def prepare(lo, hi, with_labels):
        if hi <= lo:
            return None
        chunk_source = source[:, lo:hi].reshape(-1)
        outgoing = jnp.take(blocks, chunk_source, axis=0, mode="clip")
        if with_labels:
            tile = jnp.zeros((devices_rows, 8, width), jnp.float32)
            tile = tile.at[:, 0, :per_slot].set(labels)
            outgoing = outgoing.reshape(devices_rows, (hi - lo) * block_rows, width)
            outgoing = jnp.concatenate([outgoing, tile], axis=1)
        return outgoing

    def send(lo, hi, outgoing, after, with_labels):
        if outgoing is None:
            return None, None
        if after is not None:
            outgoing = _gate(outgoing, [after])
        arrived = lax.all_to_all(outgoing, "rows", split_axis=0, concat_axis=0, tiled=True)
        if not with_labels:
            return arrived, None
        got = arrived[:, (hi - lo) * block_rows, :per_slot].astype(jnp.int32)
        data = arrived[:, : (hi - lo) * block_rows].reshape(-1, block_rows, width)
        return data, got

    def masked_gram(rows_of):
        kept = jnp.where(valid[:, None, None], rows_of.reshape(capacity, block_rows, width), 0.0)
        return (
            lax.dot_general(
                kept.reshape(-1, width),
                rows_of,
                (((0,), (0,)), ((), ())),
                precision=lax.Precision.HIGHEST,
                preferred_element_type=jnp.float32,
            )
            / total
        )

    arrived = [None, None, None]
    carrier = [k for k, (lo, hi) in enumerate(bounds) if hi > lo][-2:][0]
    outgoing = [prepare(lo, hi, carrier == k) for k, (lo, hi) in enumerate(bounds)]
    flat = blocks.reshape(-1, width)
    arrived[0], got0 = send(*bounds[0], outgoing[0], None, carrier == 0)
    gram_one = _gate(masked_gram(flat), [outgoing[1], outgoing[2]])
    reduced_one, rows_one = reduce_gram(gram_one, [arrived[0]])
    arrived[1], got1 = send(*bounds[1], outgoing[1], rows_one, carrier == 1)
    lower_one, inverse_one = factor(reduced_one)
    first_held = apply_inverse(flat, inverse_one)
    reduced_two, rows_two = reduce_gram(masked_gram(first_held), [arrived[1]])
    arrived[2], got2 = send(*bounds[2], outgoing[2], rows_two, carrier == 2)
    lower_two, inverse_two = factor(reduced_two)
    arrived_labels = [got0, got1, got2][carrier]

    wanted = own_index * BLK_DEV + jnp.arange(BLK_DEV, dtype=jnp.int32)
    combined = _mm(inverse_one.T, inverse_two.T)
    resident = None
    for (lo, hi), chunk in zip(bounds, arrived):
        if chunk is None:
            continue
        chunk_labels = arrived_labels[:, lo:hi].reshape(-1)
        pick = (chunk_labels[None, :] == wanted[:, None]).astype(jnp.float32)
        if resident is not None and chunk is arrived[2]:
            pick = _gate(pick, [resident])
        picked = lax.dot_general(
            pick,
            chunk,
            (((1,), (0,)), ((), ())),
            precision=lax.Precision.HIGHEST,
            preferred_element_type=jnp.float32,
        )
        resident = picked if resident is None else resident + picked
    resident = resident.reshape(-1, width)
    second = apply_inverse(resident, combined.T)
    result = second.reshape(BLK_DEV, block_rows, width)
    r_factor = jnp.dot(
        lower_two.T,
        lower_one.T,
        precision=lax.Precision.HIGHEST,
        preferred_element_type=jnp.float32,
    )
    return (result[:, None], r_factor)


def solution(mesh):
    in_specs = (P("rows", "sub", None, None), P("rows", "sub"), P("rows", "sub"))
    out_specs = (P("rows", "sub", None, None), P())
    return jax.shard_map(
        per_device, mesh=mesh, in_specs=in_specs, out_specs=out_specs, check_vma=False
    )
```

```python
import jax
import jax.numpy as jnp
from jax import lax
from jax.sharding import PartitionSpec as P

BLK_DEV = 32


def _mm(a, b):
    return jnp.dot(a, b, precision=lax.Precision.HIGHEST, preferred_element_type=jnp.float32)


def _lower_inverse(lower):
    identity = jnp.eye(lower.shape[0], dtype=lower.dtype)
    return lax.linalg.triangular_solve(lower, identity, left_side=True, lower=True)


def factor(gram):
    n = gram.shape[0]
    if n % 2 or n < 256:
        lower = jnp.linalg.cholesky(gram)
        return (lower, _lower_inverse(lower))
    k = n // 2
    lower_11 = jnp.linalg.cholesky(gram[:k, :k])
    inverse_11 = _lower_inverse(lower_11)
    lower_21 = _mm(gram[k:, :k], inverse_11.T)
    lower_22 = jnp.linalg.cholesky(gram[k:, k:] - _mm(lower_21, lower_21.T))
    inverse_22 = _lower_inverse(lower_22)
    inverse_21 = -_mm(inverse_22, _mm(lower_21, inverse_11))
    zeros = jnp.zeros((k, n - k), gram.dtype)
    lower = jnp.block([[lower_11, zeros], [lower_21, lower_22]])
    inverse = jnp.block([[inverse_11, zeros], [inverse_21, inverse_22]])
    return (lower, inverse)


def gram_of(flattened, total):
    return (
        lax.dot_general(
            flattened,
            flattened,
            (((0,), (0,)), ((), ())),
            precision=lax.Precision.HIGHEST,
            preferred_element_type=jnp.float32,
        )
        / total
    )


def apply_inverse(flattened, inverse):
    return jnp.dot(
        flattened, inverse.T, precision=lax.Precision.HIGHEST, preferred_element_type=jnp.float32
    )


def _xor_pairs(n, bit):
    return [(i, i ^ bit) for i in range(n)]


def _power_of_two(n):
    return n > 0 and (n & (n - 1)) == 0


def reduce_gram(partial_value, hold=None):
    n_sub = lax.axis_size("sub")
    n_rows = lax.axis_size("rows")
    width = partial_value.shape[0]
    if not (_power_of_two(n_sub) and _power_of_two(n_rows) and n_sub >= 2 and width % 2 == 0):
        total = lax.psum(_gate(partial_value, hold or []), ("rows", "sub"))
        return total, total
    half = width // 2
    h = lax.axis_index("sub") % 2
    mine = lax.dynamic_slice_in_dim(partial_value, h * half, half, 0)
    theirs = lax.dynamic_slice_in_dim(partial_value, (1 - h) * half, half, 0)
    y = mine + lax.ppermute(theirs, "sub", _xor_pairs(n_sub, 1))
    bit = 2
    while bit < n_sub:
        y = y + lax.ppermute(y, "sub", _xor_pairs(n_sub, bit))
        bit *= 2
    if hold:
        y = _gate(y, hold)
    bit = 1
    if n_rows >= 4:
        me = lax.axis_index("rows") % 4
        received = [y] + [lax.ppermute(y, "rows", _xor_pairs(n_rows, b)) for b in (1, 2, 3)]
        ordered = [lax.select_n(me ^ member, *received) for member in range(4)]
        y = ((ordered[0] + ordered[1]) + ordered[2]) + ordered[3]
        bit = 4
    while bit < n_rows:
        y = y + lax.ppermute(y, "rows", _xor_pairs(n_rows, bit))
        bit *= 2
    other = lax.ppermute(y, "sub", _xor_pairs(n_sub, 1))
    first_half = jnp.where(h == 0, y, other)
    second_half = jnp.where(h == 0, other, y)
    return jnp.concatenate([first_half, second_half], axis=0), y


def _gate(value, deps):
    flag = jnp.zeros((), jnp.bool_)
    for dep in deps:
        if dep is None:
            continue
        probe = dep[(0,) * dep.ndim]
        flag = flag | (probe != probe)
    corner = value[(slice(0, 1),) * value.ndim]
    kept = jnp.where(flag, jnp.zeros_like(corner), corner)
    return lax.dynamic_update_slice(value, kept, (0,) * value.ndim)


def per_device(held, held_block, held_count):
    capacity = held.shape[0]
    block_rows = held.shape[2]
    width = held.shape[3]
    devices_rows = lax.axis_size("rows")
    own_index = lax.axis_index("rows")
    per_slot = max(1, capacity // devices_rows)
    n_out = devices_rows * per_slot
    total = float(devices_rows * lax.axis_size("sub") * BLK_DEV * block_rows)
    blocks = held[:, 0]
    block_ids = held_block[:, 0]
    count = held_count[0, 0]
    slots = jnp.arange(capacity, dtype=jnp.int32)
    valid = slots < count

    def route(ids, filled):
        destination = ids // BLK_DEV
        earlier = (
            (destination[:, None] == destination[None, :])
            & filled[None, :]
            & (slots[None, :] < slots[:, None])
        )
        rank_within = jnp.sum(earlier.astype(jnp.int32), axis=1)
        return jnp.where(filled, destination * per_slot + rank_within, n_out)

    target = route(block_ids, valid)
    positions = jnp.arange(n_out, dtype=jnp.int32)
    match = target[None, :] == positions[:, None]
    source = jnp.sum(jnp.where(match, slots[None, :], 0), axis=1)
    source = source.reshape(devices_rows, per_slot)

    present = jnp.any(match, axis=1)
    labels = jnp.where(present, jnp.take(block_ids, jnp.sum(jnp.where(match, slots[None, :], 0), axis=1), mode="clip"), -1)
    labels = labels.reshape(devices_rows, per_slot).astype(jnp.float32)

    early = per_slot // 4
    middle = (per_slot - early) // 2
    bounds = [(0, early), (early, early + middle), (early + middle, per_slot)]

    def prepare(lo, hi, with_labels):
        if hi <= lo:
            return None
        chunk_source = source[:, lo:hi].reshape(-1)
        outgoing = jnp.take(blocks, chunk_source, axis=0, mode="clip")
        if with_labels:
            tile = jnp.zeros((devices_rows, 8, width), jnp.float32)
            tile = tile.at[:, 0, :per_slot].set(labels)
            outgoing = outgoing.reshape(devices_rows, (hi - lo) * block_rows, width)
            outgoing = jnp.concatenate([outgoing, tile], axis=1)
        return outgoing

    def send(lo, hi, outgoing, after, with_labels):
        if outgoing is None:
            return None, None
        if after is not None:
            outgoing = _gate(outgoing, [after])
        arrived = lax.all_to_all(outgoing, "rows", split_axis=0, concat_axis=0, tiled=True)
        if not with_labels:
            return arrived, None
        got = arrived[:, (hi - lo) * block_rows, :per_slot].astype(jnp.int32)
        data = arrived[:, : (hi - lo) * block_rows].reshape(-1, block_rows, width)
        return data, got

    def masked_gram(rows_of):
        kept = jnp.where(valid[:, None, None], rows_of.reshape(capacity, block_rows, width), 0.0)
        return (
            lax.dot_general(
                kept.reshape(-1, width),
                rows_of,
                (((0,), (0,)), ((), ())),
                precision=lax.Precision.HIGHEST,
                preferred_element_type=jnp.float32,
            )
            / total
        )

    arrived = [None, None, None]
    carrier = [k for k, (lo, hi) in enumerate(bounds) if hi > lo][-2:][0]
    outgoing = [prepare(lo, hi, carrier == k) for k, (lo, hi) in enumerate(bounds)]
    flat = blocks.reshape(-1, width)
    arrived[0], got0 = send(*bounds[0], outgoing[0], None, carrier == 0)
    gram_one = _gate(masked_gram(flat), [outgoing[1], outgoing[2]])
    reduced_one, rows_one = reduce_gram(gram_one, [arrived[0]])
    arrived[1], got1 = send(*bounds[1], outgoing[1], rows_one, carrier == 1)
    lower_one, inverse_one = factor(reduced_one)
    first_held = apply_inverse(flat, inverse_one)
    reduced_two, rows_two = reduce_gram(masked_gram(first_held), [arrived[1]])
    arrived[2], got2 = send(*bounds[2], outgoing[2], rows_two, carrier == 2)
    lower_two, inverse_two = factor(reduced_two)
    arrived_labels = [got0, got1, got2][carrier]

    wanted = own_index * BLK_DEV + jnp.arange(BLK_DEV, dtype=jnp.int32)
    combined = _mm(inverse_one.T, inverse_two.T)
    resident = None
    for (lo, hi), chunk in zip(bounds, arrived):
        if chunk is None:
            continue
        chunk_labels = arrived_labels[:, lo:hi].reshape(-1)
        pick = (chunk_labels[None, :] == wanted[:, None]).astype(jnp.float32)
        if resident is not None and chunk is arrived[2]:
            pick = _gate(pick, [resident])
        picked = lax.dot_general(
            pick,
            chunk,
            (((1,), (0,)), ((), ())),
            precision=lax.Precision.HIGHEST,
            preferred_element_type=jnp.float32,
        )
        resident = picked if resident is None else resident + picked
    resident = resident.reshape(-1, width)
    second = apply_inverse(resident, combined.T)
    result = second.reshape(BLK_DEV, block_rows, width)
    r_factor = jnp.dot(
        lower_two.T,
        lower_one.T,
        precision=lax.Precision.HIGHEST,
        preferred_element_type=jnp.float32,
    )
    return (result[:, None], r_factor)


def solution(mesh):
    in_specs = (P("rows", "sub", None, None), P("rows", "sub"), P("rows", "sub"))
    out_specs = (P("rows", "sub", None, None), P())
    return jax.shard_map(
        per_device, mesh=mesh, in_specs=in_specs, out_specs=out_specs, check_vma=False
    )
```

```python
import jax
import jax.numpy as jnp
from jax import lax
from jax.sharding import PartitionSpec as P

BLK_DEV = 32


def _mm(a, b):
    return jnp.dot(a, b, precision=lax.Precision.HIGHEST, preferred_element_type=jnp.float32)


def _lower_inverse(lower):
    identity = jnp.eye(lower.shape[0], dtype=lower.dtype)
    return lax.linalg.triangular_solve(lower, identity, left_side=True, lower=True)


def factor(gram):
    n = gram.shape[0]
    if n % 2 or n < 256:
        lower = jnp.linalg.cholesky(gram)
        return (lower, _lower_inverse(lower))
    k = n // 2
    lower_11 = jnp.linalg.cholesky(gram[:k, :k])
    inverse_11 = _lower_inverse(lower_11)
    lower_21 = _mm(gram[k:, :k], inverse_11.T)
    lower_22 = jnp.linalg.cholesky(gram[k:, k:] - _mm(lower_21, lower_21.T))
    inverse_22 = _lower_inverse(lower_22)
    inverse_21 = -_mm(inverse_22, _mm(lower_21, inverse_11))
    zeros = jnp.zeros((k, n - k), gram.dtype)
    lower = jnp.block([[lower_11, zeros], [lower_21, lower_22]])
    inverse = jnp.block([[inverse_11, zeros], [inverse_21, inverse_22]])
    return (lower, inverse)


def gram_of(flattened, total):
    return (
        lax.dot_general(
            flattened,
            flattened,
            (((0,), (0,)), ((), ())),
            precision=lax.Precision.HIGHEST,
            preferred_element_type=jnp.float32,
        )
        / total
    )


def apply_inverse(flattened, inverse):
    return jnp.dot(
        flattened, inverse.T, precision=lax.Precision.HIGHEST, preferred_element_type=jnp.float32
    )


def _xor_pairs(n, bit):
    return [(i, i ^ bit) for i in range(n)]


def _power_of_two(n):
    return n > 0 and (n & (n - 1)) == 0


def reduce_gram(partial_value, hold=None):
    n_sub = lax.axis_size("sub")
    n_rows = lax.axis_size("rows")
    width = partial_value.shape[0]
    if not (_power_of_two(n_sub) and _power_of_two(n_rows) and n_sub >= 2 and width % 2 == 0):
        total = lax.psum(_gate(partial_value, hold or []), ("rows", "sub"))
        return total, total
    half = width // 2
    h = lax.axis_index("sub") % 2
    mine = lax.dynamic_slice_in_dim(partial_value, h * half, half, 0)
    theirs = lax.dynamic_slice_in_dim(partial_value, (1 - h) * half, half, 0)
    y = mine + lax.ppermute(theirs, "sub", _xor_pairs(n_sub, 1))
    bit = 2
    while bit < n_sub:
        y = y + lax.ppermute(y, "sub", _xor_pairs(n_sub, bit))
        bit *= 2
    if hold:
        y = jnp.where(_flag(hold), jnp.zeros_like(y), y)
    bit = 1
    while bit < n_rows:
        y = y + lax.ppermute(y, "rows", _xor_pairs(n_rows, bit))
        bit *= 2
    other = lax.ppermute(y, "sub", _xor_pairs(n_sub, 1))
    first_half = jnp.where(h == 0, y, other)
    second_half = jnp.where(h == 0, other, y)
    return jnp.concatenate([first_half, second_half], axis=0), y


def _flag(deps):
    flag = jnp.zeros((), jnp.bool_)
    for dep in deps:
        if dep is None:
            continue
        probe = dep[(0,) * dep.ndim]
        flag = flag | (probe != probe)
    return flag


def _gate(value, deps):
    flag = _flag(deps)
    corner = value[(slice(0, 1),) * value.ndim]
    kept = jnp.where(flag, jnp.zeros_like(corner), corner)
    return lax.dynamic_update_slice(value, kept, (0,) * value.ndim)


def per_device(held, held_block, held_count):
    capacity = held.shape[0]
    block_rows = held.shape[2]
    width = held.shape[3]
    devices_rows = lax.axis_size("rows")
    own_index = lax.axis_index("rows")
    per_slot = max(1, capacity // devices_rows)
    n_out = devices_rows * per_slot
    total = float(devices_rows * lax.axis_size("sub") * BLK_DEV * block_rows)
    blocks = held[:, 0]
    block_ids = held_block[:, 0]
    count = held_count[0, 0]
    slots = jnp.arange(capacity, dtype=jnp.int32)
    valid = slots < count

    def route(ids, filled):
        destination = ids // BLK_DEV
        earlier = (
            (destination[:, None] == destination[None, :])
            & filled[None, :]
            & (slots[None, :] < slots[:, None])
        )
        rank_within = jnp.sum(earlier.astype(jnp.int32), axis=1)
        return jnp.where(filled, destination * per_slot + rank_within, n_out)

    target = route(block_ids, valid)
    positions = jnp.arange(n_out, dtype=jnp.int32)
    match = target[None, :] == positions[:, None]
    source = jnp.sum(jnp.where(match, slots[None, :], 0), axis=1)
    source = source.reshape(devices_rows, per_slot)

    present = jnp.any(match, axis=1)
    labels = jnp.where(present, jnp.take(block_ids, jnp.sum(jnp.where(match, slots[None, :], 0), axis=1), mode="clip"), -1)
    labels = labels.reshape(devices_rows, per_slot).astype(jnp.float32)

    early = per_slot // 4
    middle = (per_slot - early) // 2
    bounds = [(0, early), (early, early + middle), (early + middle, per_slot)]

    def prepare(lo, hi, with_labels):
        if hi <= lo:
            return None
        chunk_source = source[:, lo:hi].reshape(-1)
        outgoing = jnp.take(blocks, chunk_source, axis=0, mode="clip")
        if with_labels:
            tile = jnp.zeros((devices_rows, 8, width), jnp.float32)
            tile = tile.at[:, 0, :per_slot].set(labels)
            outgoing = outgoing.reshape(devices_rows, (hi - lo) * block_rows, width)
            outgoing = jnp.concatenate([outgoing, tile], axis=1)
        return outgoing

    def send(lo, hi, outgoing, after, with_labels):
        if outgoing is None:
            return None, None
        if after is not None:
            outgoing = _gate(outgoing, [after])
        arrived = lax.all_to_all(outgoing, "rows", split_axis=0, concat_axis=0, tiled=True)
        if not with_labels:
            return arrived, None
        got = arrived[:, (hi - lo) * block_rows, :per_slot].astype(jnp.int32)
        data = arrived[:, : (hi - lo) * block_rows].reshape(-1, block_rows, width)
        return data, got

    def masked_gram(rows_of):
        kept = jnp.where(valid[:, None, None], rows_of.reshape(capacity, block_rows, width), 0.0)
        return (
            lax.dot_general(
                kept.reshape(-1, width),
                rows_of,
                (((0,), (0,)), ((), ())),
                precision=lax.Precision.HIGHEST,
                preferred_element_type=jnp.float32,
            )
            / total
        )

    arrived = [None, None, None]
    carrier = [k for k, (lo, hi) in enumerate(bounds) if hi > lo][-2:][0]
    outgoing = [prepare(lo, hi, carrier == k) for k, (lo, hi) in enumerate(bounds)]
    flat = blocks.reshape(-1, width)
    arrived[0], got0 = send(*bounds[0], outgoing[0], None, carrier == 0)
    gram_one = _gate(masked_gram(flat), [outgoing[1], outgoing[2]])
    reduced_one, rows_one = reduce_gram(gram_one, [arrived[0]])
    arrived[1], got1 = send(*bounds[1], outgoing[1], rows_one, carrier == 1)
    lower_one, inverse_one = factor(reduced_one)
    first_held = apply_inverse(flat, inverse_one)
    reduced_two, rows_two = reduce_gram(masked_gram(first_held), [arrived[1]])
    arrived[2], got2 = send(*bounds[2], outgoing[2], rows_two, carrier == 2)
    lower_two, inverse_two = factor(reduced_two)
    arrived_labels = [got0, got1, got2][carrier]

    wanted = own_index * BLK_DEV + jnp.arange(BLK_DEV, dtype=jnp.int32)
    combined = _mm(inverse_one.T, inverse_two.T)
    resident = None
    for (lo, hi), chunk in zip(bounds, arrived):
        if chunk is None:
            continue
        chunk_labels = arrived_labels[:, lo:hi].reshape(-1)
        pick = (chunk_labels[None, :] == wanted[:, None]).astype(jnp.float32)
        if resident is not None and chunk is arrived[2]:
            pick = _gate(pick, [resident])
        picked = lax.dot_general(
            pick,
            chunk,
            (((1,), (0,)), ((), ())),
            precision=lax.Precision.HIGHEST,
            preferred_element_type=jnp.float32,
        )
        resident = picked if resident is None else resident + picked
    resident = resident.reshape(-1, width)
    second = apply_inverse(resident, combined.T)
    result = second.reshape(BLK_DEV, block_rows, width)
    r_factor = jnp.dot(
        lower_two.T,
        lower_one.T,
        precision=lax.Precision.HIGHEST,
        preferred_element_type=jnp.float32,
    )
    return (result[:, None], r_factor)


def solution(mesh):
    in_specs = (P("rows", "sub", None, None), P("rows", "sub"), P("rows", "sub"))
    out_specs = (P("rows", "sub", None, None), P())
    return jax.shard_map(
        per_device, mesh=mesh, in_specs=in_specs, out_specs=out_specs, check_vma=False
    )
```

```python
import jax
import jax.numpy as jnp
from jax import lax
from jax.sharding import PartitionSpec as P

BLK_DEV = 32


def _mm(a, b):
    return jnp.dot(a, b, precision=lax.Precision.HIGHEST, preferred_element_type=jnp.float32)


def _lower_inverse(lower):
    identity = jnp.eye(lower.shape[0], dtype=lower.dtype)
    return lax.linalg.triangular_solve(lower, identity, left_side=True, lower=True)


def factor(gram):
    n = gram.shape[0]
    if n % 2 or n < 256:
        lower = jnp.linalg.cholesky(gram)
        return (lower, _lower_inverse(lower))
    k = n // 2
    lower_11 = jnp.linalg.cholesky(gram[:k, :k])
    inverse_11 = _lower_inverse(lower_11)
    lower_21 = _mm(gram[k:, :k], inverse_11.T)
    lower_22 = jnp.linalg.cholesky(gram[k:, k:] - _mm(lower_21, lower_21.T))
    inverse_22 = _lower_inverse(lower_22)
    inverse_21 = -_mm(inverse_22, _mm(lower_21, inverse_11))
    zeros = jnp.zeros((k, n - k), gram.dtype)
    lower = jnp.block([[lower_11, zeros], [lower_21, lower_22]])
    inverse = jnp.block([[inverse_11, zeros], [inverse_21, inverse_22]])
    return (lower, inverse)


def gram_of(flattened, total):
    return (
        lax.dot_general(
            flattened,
            flattened,
            (((0,), (0,)), ((), ())),
            precision=lax.Precision.HIGHEST,
            preferred_element_type=jnp.float32,
        )
        / total
    )


def apply_inverse(flattened, inverse):
    return jnp.dot(
        flattened, inverse.T, precision=lax.Precision.HIGHEST, preferred_element_type=jnp.float32
    )


def _xor_pairs(n, bit):
    return [(i, i ^ bit) for i in range(n)]


def _power_of_two(n):
    return n > 0 and (n & (n - 1)) == 0


def reduce_gram(partial_value, hold=None):
    n_sub = lax.axis_size("sub")
    n_rows = lax.axis_size("rows")
    width = partial_value.shape[0]
    if not (_power_of_two(n_sub) and _power_of_two(n_rows) and n_sub >= 2 and width % 2 == 0):
        total = lax.psum(_gate(partial_value, hold or []), ("rows", "sub"))
        return total, total
    half = width // 2
    h = lax.axis_index("sub") % 2
    mine = lax.dynamic_slice_in_dim(partial_value, h * half, half, 0)
    theirs = lax.dynamic_slice_in_dim(partial_value, (1 - h) * half, half, 0)
    y = mine + lax.ppermute(theirs, "sub", _xor_pairs(n_sub, 1))
    bit = 2
    while bit < n_sub:
        y = y + lax.ppermute(y, "sub", _xor_pairs(n_sub, bit))
        bit *= 2
    if hold:
        y = jnp.where(_flag(hold), jnp.zeros_like(y), y)
    bit = 1
    while bit < n_rows:
        y = y + lax.ppermute(y, "rows", _xor_pairs(n_rows, bit))
        bit *= 2
    other = lax.ppermute(y, "sub", _xor_pairs(n_sub, 1))
    first_half = jnp.where(h == 0, y, other)
    second_half = jnp.where(h == 0, other, y)
    return jnp.concatenate([first_half, second_half], axis=0), y


def _flag(deps):
    flag = jnp.zeros((), jnp.bool_)
    for dep in deps:
        if dep is None:
            continue
        probe = dep[(0,) * dep.ndim]
        flag = flag | (probe != probe)
    return flag


def _gate(value, deps):
    flag = _flag(deps)
    corner = value[(slice(0, 1),) * value.ndim]
    kept = jnp.where(flag, jnp.zeros_like(corner), corner)
    return lax.dynamic_update_slice(value, kept, (0,) * value.ndim)


def per_device(held, held_block, held_count):
    capacity = held.shape[0]
    block_rows = held.shape[2]
    width = held.shape[3]
    devices_rows = lax.axis_size("rows")
    own_index = lax.axis_index("rows")
    per_slot = max(1, capacity // devices_rows)
    n_out = devices_rows * per_slot
    total = float(devices_rows * lax.axis_size("sub") * BLK_DEV * block_rows)
    blocks = held[:, 0]
    block_ids = held_block[:, 0]
    count = held_count[0, 0]
    slots = jnp.arange(capacity, dtype=jnp.int32)
    valid = slots < count

    def route(ids, filled):
        destination = ids // BLK_DEV
        earlier = (
            (destination[:, None] == destination[None, :])
            & filled[None, :]
            & (slots[None, :] < slots[:, None])
        )
        rank_within = jnp.sum(earlier.astype(jnp.int32), axis=1)
        return jnp.where(filled, destination * per_slot + rank_within, n_out)

    target = route(block_ids, valid)
    positions = jnp.arange(n_out, dtype=jnp.int32)
    match = target[None, :] == positions[:, None]
    source = jnp.sum(jnp.where(match, slots[None, :], 0), axis=1)
    source = source.reshape(devices_rows, per_slot)

    present = jnp.any(match, axis=1)
    labels = jnp.where(present, jnp.take(block_ids, jnp.sum(jnp.where(match, slots[None, :], 0), axis=1), mode="clip"), -1)
    labels = labels.reshape(devices_rows, per_slot).astype(jnp.float32)

    halves = 2 if block_rows % 16 == 0 else 1
    piece_rows = block_rows // halves
    ranks = per_slot * halves
    pieces = blocks.reshape(capacity * halves, piece_rows, width)
    piece_source = (source[:, :, None] * halves + jnp.arange(halves, dtype=jnp.int32)).reshape(
        devices_rows, ranks
    )
    early = (3 * ranks) // 16
    middle = (7 * ranks) // 16
    bounds = [(0, early), (early, early + middle), (early + middle, ranks)]

    def prepare(lo, hi, with_labels):
        if hi <= lo:
            return None
        chunk_source = piece_source[:, lo:hi].reshape(-1)
        outgoing = jnp.take(pieces, chunk_source, axis=0, mode="clip")
        if with_labels:
            tile = jnp.zeros((devices_rows, 8, width), jnp.float32)
            tile = tile.at[:, 0, :per_slot].set(labels)
            outgoing = outgoing.reshape(devices_rows, (hi - lo) * piece_rows, width)
            outgoing = jnp.concatenate([outgoing, tile], axis=1)
        return outgoing

    def send(lo, hi, outgoing, after, with_labels):
        if outgoing is None:
            return None, None
        if after is not None:
            outgoing = _gate(outgoing, [after])
        arrived = lax.all_to_all(outgoing, "rows", split_axis=0, concat_axis=0, tiled=True)
        if not with_labels:
            return arrived, None
        got = arrived[:, (hi - lo) * piece_rows, :per_slot].astype(jnp.int32)
        data = arrived[:, : (hi - lo) * piece_rows].reshape(-1, piece_rows, width)
        return data, got

    def masked_gram(rows_of):
        kept = jnp.where(valid[:, None, None], rows_of.reshape(capacity, block_rows, width), 0.0)
        return (
            lax.dot_general(
                kept.reshape(-1, width),
                rows_of,
                (((0,), (0,)), ((), ())),
                precision=lax.Precision.HIGHEST,
                preferred_element_type=jnp.float32,
            )
            / total
        )

    arrived = [None, None, None]
    carrier = [k for k, (lo, hi) in enumerate(bounds) if hi > lo][-2:][0]
    outgoing = [prepare(lo, hi, carrier == k) for k, (lo, hi) in enumerate(bounds)]
    flat = blocks.reshape(-1, width)
    arrived[0], got0 = send(*bounds[0], outgoing[0], None, carrier == 0)
    gram_one = _gate(masked_gram(flat), [outgoing[1], outgoing[2]])
    reduced_one, rows_one = reduce_gram(gram_one, [arrived[0]])
    arrived[1], got1 = send(*bounds[1], outgoing[1], rows_one, carrier == 1)
    lower_one, inverse_one = factor(reduced_one)
    first_held = apply_inverse(flat, inverse_one)
    reduced_two, rows_two = reduce_gram(masked_gram(first_held), [arrived[1]])
    arrived[2], got2 = send(*bounds[2], outgoing[2], rows_two, carrier == 2)
    lower_two, inverse_two = factor(reduced_two)
    arrived_labels = [got0, got1, got2][carrier]

    wanted = own_index * BLK_DEV * halves + jnp.arange(BLK_DEV * halves, dtype=jnp.int32)
    piece_labels = jnp.where(
        arrived_labels[:, :, None] >= 0,
        arrived_labels[:, :, None] * halves + jnp.arange(halves, dtype=jnp.int32),
        -1,
    ).reshape(devices_rows, ranks)
    combined = _mm(inverse_one.T, inverse_two.T)
    resident = None
    for (lo, hi), chunk in zip(bounds, arrived):
        if chunk is None:
            continue
        chunk_labels = piece_labels[:, lo:hi].reshape(-1)
        pick = (chunk_labels[None, :] == wanted[:, None]).astype(jnp.float32)
        if resident is not None and chunk is arrived[2]:
            pick = _gate(pick, [resident])
        picked = lax.dot_general(
            pick,
            chunk,
            (((1,), (0,)), ((), ())),
            precision=lax.Precision.HIGHEST,
            preferred_element_type=jnp.float32,
        )
        resident = picked if resident is None else resident + picked
    resident = resident.reshape(-1, width)
    second = apply_inverse(resident, combined.T)
    result = second.reshape(BLK_DEV, block_rows, width)
    r_factor = jnp.dot(
        lower_two.T,
        lower_one.T,
        precision=lax.Precision.HIGHEST,
        preferred_element_type=jnp.float32,
    )
    return (result[:, None], r_factor)


def solution(mesh):
    in_specs = (P("rows", "sub", None, None), P("rows", "sub"), P("rows", "sub"))
    out_specs = (P("rows", "sub", None, None), P())
    return jax.shard_map(
        per_device, mesh=mesh, in_specs=in_specs, out_specs=out_specs, check_vma=False
    )
```

```python
import jax
import jax.numpy as jnp
from jax import lax
from jax.sharding import PartitionSpec as P

BLK_DEV = 32


def _mm(a, b):
    return jnp.dot(a, b, precision=lax.Precision.HIGHEST, preferred_element_type=jnp.float32)


def _lower_inverse(lower):
    identity = jnp.eye(lower.shape[0], dtype=lower.dtype)
    return lax.linalg.triangular_solve(lower, identity, left_side=True, lower=True)


def factor(gram):
    n = gram.shape[0]
    if n % 2 or n < 256:
        lower = jnp.linalg.cholesky(gram)
        return (lower, _lower_inverse(lower))
    k = n // 2
    lower_11 = jnp.linalg.cholesky(gram[:k, :k])
    inverse_11 = _lower_inverse(lower_11)
    lower_21 = _mm(gram[k:, :k], inverse_11.T)
    lower_22 = jnp.linalg.cholesky(gram[k:, k:] - _mm(lower_21, lower_21.T))
    inverse_22 = _lower_inverse(lower_22)
    inverse_21 = -_mm(inverse_22, _mm(lower_21, inverse_11))
    zeros = jnp.zeros((k, n - k), gram.dtype)
    lower = jnp.block([[lower_11, zeros], [lower_21, lower_22]])
    inverse = jnp.block([[inverse_11, zeros], [inverse_21, inverse_22]])
    return (lower, inverse)


def gram_of(flattened, total):
    return (
        lax.dot_general(
            flattened,
            flattened,
            (((0,), (0,)), ((), ())),
            precision=lax.Precision.HIGHEST,
            preferred_element_type=jnp.float32,
        )
        / total
    )


def apply_inverse(flattened, inverse):
    return jnp.dot(
        flattened, inverse.T, precision=lax.Precision.HIGHEST, preferred_element_type=jnp.float32
    )


def _xor_pairs(n, bit):
    return [(i, i ^ bit) for i in range(n)]


def _power_of_two(n):
    return n > 0 and (n & (n - 1)) == 0


def reduce_gram(partial_value, hold=None):
    n_sub = lax.axis_size("sub")
    n_rows = lax.axis_size("rows")
    width = partial_value.shape[0]
    if not (_power_of_two(n_sub) and _power_of_two(n_rows) and n_sub >= 2 and width % 2 == 0):
        total = lax.psum(_gate(partial_value, hold or []), ("rows", "sub"))
        return total, total
    half = width // 2
    h = lax.axis_index("sub") % 2
    mine = lax.dynamic_slice_in_dim(partial_value, h * half, half, 0)
    theirs = lax.dynamic_slice_in_dim(partial_value, (1 - h) * half, half, 0)
    y = mine + lax.ppermute(theirs, "sub", _xor_pairs(n_sub, 1))
    bit = 2
    while bit < n_sub:
        y = y + lax.ppermute(y, "sub", _xor_pairs(n_sub, bit))
        bit *= 2
    if hold:
        y = jnp.where(_flag(hold), jnp.zeros_like(y), y)
    bit = 1
    while bit < n_rows:
        y = y + lax.ppermute(y, "rows", _xor_pairs(n_rows, bit))
        bit *= 2
    other = lax.ppermute(y, "sub", _xor_pairs(n_sub, 1))
    first_half = jnp.where(h == 0, y, other)
    second_half = jnp.where(h == 0, other, y)
    return jnp.concatenate([first_half, second_half], axis=0), y


def _flag(deps):
    flag = jnp.zeros((), jnp.bool_)
    for dep in deps:
        if dep is None:
            continue
        probe = dep[(0,) * dep.ndim]
        flag = flag | (probe != probe)
    return flag


def _gate(value, deps):
    flag = _flag(deps)
    corner = value[(slice(0, 1),) * value.ndim]
    kept = jnp.where(flag, jnp.zeros_like(corner), corner)
    return lax.dynamic_update_slice(value, kept, (0,) * value.ndim)


def per_device(held, held_block, held_count):
    capacity = held.shape[0]
    block_rows = held.shape[2]
    width = held.shape[3]
    devices_rows = lax.axis_size("rows")
    own_index = lax.axis_index("rows")
    per_slot = max(1, capacity // devices_rows)
    n_out = devices_rows * per_slot
    total = float(devices_rows * lax.axis_size("sub") * BLK_DEV * block_rows)
    blocks = held[:, 0]
    block_ids = held_block[:, 0]
    count = held_count[0, 0]
    slots = jnp.arange(capacity, dtype=jnp.int32)
    valid = slots < count

    def route(ids, filled):
        destination = ids // BLK_DEV
        earlier = (
            (destination[:, None] == destination[None, :])
            & filled[None, :]
            & (slots[None, :] < slots[:, None])
        )
        rank_within = jnp.sum(earlier.astype(jnp.int32), axis=1)
        return jnp.where(filled, destination * per_slot + rank_within, n_out)

    target = route(block_ids, valid)
    positions = jnp.arange(n_out, dtype=jnp.int32)
    match = target[None, :] == positions[:, None]
    source = jnp.sum(jnp.where(match, slots[None, :], 0), axis=1)
    source = source.reshape(devices_rows, per_slot)

    present = jnp.any(match, axis=1)
    labels = jnp.where(present, jnp.take(block_ids, jnp.sum(jnp.where(match, slots[None, :], 0), axis=1), mode="clip"), -1)
    labels = labels.reshape(devices_rows, per_slot).astype(jnp.float32)

    early = per_slot // 4
    middle = (per_slot - early) // 2
    bounds = [(0, early), (early, early + middle), (early + middle, per_slot)]

    def prepare(lo, hi, with_labels):
        if hi <= lo:
            return None
        chunk_source = source[:, lo:hi].reshape(-1)
        outgoing = jnp.take(blocks, chunk_source, axis=0, mode="clip")
        if with_labels:
            tile = jnp.zeros((devices_rows, 8, width), jnp.float32)
            tile = tile.at[:, 0, :per_slot].set(labels)
            outgoing = outgoing.reshape(devices_rows, (hi - lo) * block_rows, width)
            outgoing = jnp.concatenate([outgoing, tile], axis=1)
        return outgoing

    def send(lo, hi, outgoing, after, with_labels):
        if outgoing is None:
            return None, None
        if after is not None:
            outgoing = _gate(outgoing, [after])
        arrived = lax.all_to_all(outgoing, "rows", split_axis=0, concat_axis=0, tiled=True)
        if not with_labels:
            return arrived, None
        got = arrived[:, (hi - lo) * block_rows, :per_slot]
        data = arrived[:, : (hi - lo) * block_rows].reshape(-1, block_rows, width)
        return data, got

    def masked_gram(rows_of):
        kept = jnp.where(valid[:, None, None], rows_of.reshape(capacity, block_rows, width), 0.0)
        return (
            lax.dot_general(
                kept.reshape(-1, width),
                rows_of,
                (((0,), (0,)), ((), ())),
                precision=lax.Precision.HIGHEST,
                preferred_element_type=jnp.float32,
            )
            / total
        )

    arrived = [None, None, None]
    carrier = [k for k, (lo, hi) in enumerate(bounds) if hi > lo][-2:][0]
    outgoing = [prepare(lo, hi, carrier == k) for k, (lo, hi) in enumerate(bounds)]
    flat = blocks.reshape(-1, width)
    arrived[0], got0 = send(*bounds[0], outgoing[0], None, carrier == 0)
    gram_one = _gate(masked_gram(flat), [outgoing[1], outgoing[2]])
    reduced_one, rows_one = reduce_gram(gram_one, [arrived[0]])
    arrived[1], got1 = send(*bounds[1], outgoing[1], rows_one, carrier == 1)
    lower_one, inverse_one = factor(reduced_one)
    first_held = apply_inverse(flat, inverse_one)
    landed = got1 if carrier == 1 else arrived[1]
    reduced_two, rows_two = reduce_gram(masked_gram(first_held), [landed])
    arrived[2], got2 = send(*bounds[2], outgoing[2], rows_two, carrier == 2)
    lower_two, inverse_two = factor(reduced_two)
    arrived_labels = [got0, got1, got2][carrier].astype(jnp.int32)

    wanted = own_index * BLK_DEV + jnp.arange(BLK_DEV, dtype=jnp.int32)
    combined = _mm(inverse_one.T, inverse_two.T)
    resident = None
    for (lo, hi), chunk in zip(bounds, arrived):
        if chunk is None:
            continue
        chunk_labels = arrived_labels[:, lo:hi].reshape(-1)
        pick = (chunk_labels[None, :] == wanted[:, None]).astype(jnp.float32)
        if resident is not None and chunk is arrived[2]:
            pick = _gate(pick, [resident])
        picked = lax.dot_general(
            pick,
            chunk,
            (((1,), (0,)), ((), ())),
            precision=lax.Precision.HIGHEST,
            preferred_element_type=jnp.float32,
        )
        resident = picked if resident is None else resident + picked
    resident = resident.reshape(-1, width)
    second = apply_inverse(resident, combined.T)
    result = second.reshape(BLK_DEV, block_rows, width)
    r_factor = jnp.dot(
        lower_two.T,
        lower_one.T,
        precision=lax.Precision.HIGHEST,
        preferred_element_type=jnp.float32,
    )
    return (result[:, None], r_factor)


def solution(mesh):
    in_specs = (P("rows", "sub", None, None), P("rows", "sub"), P("rows", "sub"))
    out_specs = (P("rows", "sub", None, None), P())
    return jax.shard_map(
        per_device, mesh=mesh, in_specs=in_specs, out_specs=out_specs, check_vma=False
    )
```

```python
import jax
import jax.numpy as jnp
from jax import lax
from jax.sharding import PartitionSpec as P

BLK_DEV = 32


def _mm(a, b):
    return jnp.dot(a, b, precision=lax.Precision.HIGHEST, preferred_element_type=jnp.float32)


def _lower_inverse(lower):
    identity = jnp.eye(lower.shape[0], dtype=lower.dtype)
    return lax.linalg.triangular_solve(lower, identity, left_side=True, lower=True)


def factor(gram):
    n = gram.shape[0]
    if n % 2 or n < 256:
        lower = jnp.linalg.cholesky(gram)
        return (lower, _lower_inverse(lower))
    k = n // 2
    lower_11 = lax.linalg.cholesky(gram[:k, :k], symmetrize_input=False)
    inverse_11 = _lower_inverse(lower_11)
    lower_21 = _mm(gram[k:, :k], inverse_11.T)
    lower_22 = lax.linalg.cholesky(gram[k:, k:] - _mm(lower_21, lower_21.T), symmetrize_input=False)
    inverse_22 = _lower_inverse(lower_22)
    inverse_21 = -_mm(inverse_22, _mm(lower_21, inverse_11))
    zeros = jnp.zeros((k, n - k), gram.dtype)
    lower = jnp.block([[lower_11, zeros], [lower_21, lower_22]])
    inverse = jnp.block([[inverse_11, zeros], [inverse_21, inverse_22]])
    return (lower, inverse)


def gram_of(flattened, total):
    return (
        lax.dot_general(
            flattened,
            flattened,
            (((0,), (0,)), ((), ())),
            precision=lax.Precision.HIGHEST,
            preferred_element_type=jnp.float32,
        )
        / total
    )


def apply_inverse(flattened, inverse):
    return jnp.dot(
        flattened, inverse.T, precision=lax.Precision.HIGHEST, preferred_element_type=jnp.float32
    )


def _xor_pairs(n, bit):
    return [(i, i ^ bit) for i in range(n)]


def _power_of_two(n):
    return n > 0 and (n & (n - 1)) == 0


def reduce_gram(partial_value, hold=None):
    n_sub = lax.axis_size("sub")
    n_rows = lax.axis_size("rows")
    width = partial_value.shape[0]
    if not (_power_of_two(n_sub) and _power_of_two(n_rows) and n_sub >= 2 and width % 2 == 0):
        total = lax.psum(_gate(partial_value, hold or []), ("rows", "sub"))
        return total, total
    half = width // 2
    h = lax.axis_index("sub") % 2
    mine = lax.dynamic_slice_in_dim(partial_value, h * half, half, 0)
    theirs = lax.dynamic_slice_in_dim(partial_value, (1 - h) * half, half, 0)
    y = mine + lax.ppermute(theirs, "sub", _xor_pairs(n_sub, 1))
    bit = 2
    while bit < n_sub:
        y = y + lax.ppermute(y, "sub", _xor_pairs(n_sub, bit))
        bit *= 2
    if hold:
        y = jnp.where(_flag(hold), jnp.zeros_like(y), y)
    bit = 1
    while bit < n_rows:
        y = y + lax.ppermute(y, "rows", _xor_pairs(n_rows, bit))
        bit *= 2
    other = lax.ppermute(y, "sub", _xor_pairs(n_sub, 1))
    first_half = jnp.where(h == 0, y, other)
    second_half = jnp.where(h == 0, other, y)
    return jnp.concatenate([first_half, second_half], axis=0), y


def _flag(deps):
    flag = jnp.zeros((), jnp.bool_)
    for dep in deps:
        if dep is None:
            continue
        probe = dep[(0,) * dep.ndim]
        flag = flag | (probe != probe)
    return flag


def _gate(value, deps):
    flag = _flag(deps)
    corner = value[(slice(0, 1),) * value.ndim]
    kept = jnp.where(flag, jnp.zeros_like(corner), corner)
    return lax.dynamic_update_slice(value, kept, (0,) * value.ndim)


def per_device(held, held_block, held_count):
    capacity = held.shape[0]
    block_rows = held.shape[2]
    width = held.shape[3]
    devices_rows = lax.axis_size("rows")
    own_index = lax.axis_index("rows")
    per_slot = max(1, capacity // devices_rows)
    n_out = devices_rows * per_slot
    total = float(devices_rows * lax.axis_size("sub") * BLK_DEV * block_rows)
    blocks = held[:, 0]
    block_ids = held_block[:, 0]
    count = held_count[0, 0]
    slots = jnp.arange(capacity, dtype=jnp.int32)
    valid = slots < count

    def route(ids, filled):
        destination = ids // BLK_DEV
        earlier = (
            (destination[:, None] == destination[None, :])
            & filled[None, :]
            & (slots[None, :] < slots[:, None])
        )
        rank_within = jnp.sum(earlier.astype(jnp.int32), axis=1)
        return jnp.where(filled, destination * per_slot + rank_within, n_out)

    target = route(block_ids, valid)
    positions = jnp.arange(n_out, dtype=jnp.int32)
    match = target[None, :] == positions[:, None]
    source = jnp.sum(jnp.where(match, slots[None, :], 0), axis=1)
    source = source.reshape(devices_rows, per_slot)

    present = jnp.any(match, axis=1)
    labels = jnp.where(present, jnp.take(block_ids, jnp.sum(jnp.where(match, slots[None, :], 0), axis=1), mode="clip"), -1)
    labels = labels.reshape(devices_rows, per_slot).astype(jnp.float32)

    early = per_slot // 4
    middle = (per_slot - early) // 2
    bounds = [(0, early), (early, early + middle), (early + middle, per_slot)]

    def prepare(lo, hi, with_labels):
        if hi <= lo:
            return None
        chunk_source = source[:, lo:hi].reshape(-1)
        outgoing = jnp.take(blocks, chunk_source, axis=0, mode="clip")
        if with_labels:
            tile = jnp.zeros((devices_rows, 8, width), jnp.float32)
            tile = tile.at[:, 0, :per_slot].set(labels)
            outgoing = outgoing.reshape(devices_rows, (hi - lo) * block_rows, width)
            outgoing = jnp.concatenate([outgoing, tile], axis=1)
        return outgoing

    def send(lo, hi, outgoing, after, with_labels):
        if outgoing is None:
            return None, None
        if after is not None:
            outgoing = _gate(outgoing, [after])
        arrived = lax.all_to_all(outgoing, "rows", split_axis=0, concat_axis=0, tiled=True)
        if not with_labels:
            return arrived, None
        got = arrived[:, (hi - lo) * block_rows, :per_slot]
        data = arrived[:, : (hi - lo) * block_rows].reshape(-1, block_rows, width)
        return data, got

    def masked_gram(rows_of):
        kept = jnp.where(valid[:, None, None], rows_of.reshape(capacity, block_rows, width), 0.0)
        return (
            lax.dot_general(
                kept.reshape(-1, width),
                rows_of,
                (((0,), (0,)), ((), ())),
                precision=lax.Precision.HIGHEST,
                preferred_element_type=jnp.float32,
            )
            / total
        )

    arrived = [None, None, None]
    carrier = [k for k, (lo, hi) in enumerate(bounds) if hi > lo][-2:][0]
    outgoing = [prepare(lo, hi, carrier == k) for k, (lo, hi) in enumerate(bounds)]
    flat = blocks.reshape(-1, width)
    arrived[0], got0 = send(*bounds[0], outgoing[0], None, carrier == 0)
    gram_one = _gate(masked_gram(flat), [outgoing[1], outgoing[2]])
    reduced_one, rows_one = reduce_gram(gram_one, [arrived[0]])
    arrived[1], got1 = send(*bounds[1], outgoing[1], rows_one, carrier == 1)
    lower_one, inverse_one = factor(reduced_one)
    first_held = apply_inverse(flat, inverse_one)
    landed = got1 if carrier == 1 else arrived[1]
    reduced_two, rows_two = reduce_gram(masked_gram(first_held), [landed])
    arrived[2], got2 = send(*bounds[2], outgoing[2], rows_two, carrier == 2)
    lower_two, inverse_two = factor(reduced_two)
    arrived_labels = [got0, got1, got2][carrier].astype(jnp.int32)

    wanted = own_index * BLK_DEV + jnp.arange(BLK_DEV, dtype=jnp.int32)
    combined = _mm(inverse_one.T, inverse_two.T)
    resident = None
    for (lo, hi), chunk in zip(bounds, arrived):
        if chunk is None:
            continue
        chunk_labels = arrived_labels[:, lo:hi].reshape(-1)
        pick = (chunk_labels[None, :] == wanted[:, None]).astype(jnp.float32)
        if resident is not None and chunk is arrived[2]:
            pick = _gate(pick, [resident])
        picked = lax.dot_general(
            pick,
            chunk,
            (((1,), (0,)), ((), ())),
            precision=lax.Precision.HIGHEST,
            preferred_element_type=jnp.float32,
        )
        resident = picked if resident is None else resident + picked
    resident = resident.reshape(-1, width)
    second = apply_inverse(resident, combined.T)
    result = second.reshape(BLK_DEV, block_rows, width)
    r_factor = jnp.dot(
        lower_two.T,
        lower_one.T,
        precision=lax.Precision.HIGHEST,
        preferred_element_type=jnp.float32,
    )
    return (result[:, None], r_factor)


def solution(mesh):
    in_specs = (P("rows", "sub", None, None), P("rows", "sub"), P("rows", "sub"))
    out_specs = (P("rows", "sub", None, None), P())
    return jax.shard_map(
        per_device, mesh=mesh, in_specs=in_specs, out_specs=out_specs, check_vma=False
    )
```

```python
import jax
import jax.numpy as jnp
from jax import lax
from jax.sharding import PartitionSpec as P

BLK_DEV = 32


def _mm(a, b):
    return jnp.dot(a, b, precision=lax.Precision.HIGHEST, preferred_element_type=jnp.float32)


def _lower_inverse(lower):
    identity = jnp.eye(lower.shape[0], dtype=lower.dtype)
    return lax.linalg.triangular_solve(lower, identity, left_side=True, lower=True)


def factor(gram):
    n = gram.shape[0]
    if n % 2 or n < 256:
        lower = jnp.linalg.cholesky(gram)
        return (lower, _lower_inverse(lower))
    k = n // 2
    lower_11 = jnp.linalg.cholesky(gram[:k, :k])
    inverse_11 = _lower_inverse(lower_11)
    lower_21 = _mm(gram[k:, :k], inverse_11.T)
    lower_22 = jnp.linalg.cholesky(gram[k:, k:] - _mm(lower_21, lower_21.T))
    inverse_22 = _lower_inverse(lower_22)
    inverse_21 = -_mm(inverse_22, _mm(lower_21, inverse_11))
    zeros = jnp.zeros((k, n - k), gram.dtype)
    lower = jnp.block([[lower_11, zeros], [lower_21, lower_22]])
    inverse = jnp.block([[inverse_11, zeros], [inverse_21, inverse_22]])
    return (lower, inverse)


def gram_of(flattened, total):
    return (
        lax.dot_general(
            flattened,
            flattened,
            (((0,), (0,)), ((), ())),
            precision=lax.Precision.HIGHEST,
            preferred_element_type=jnp.float32,
        )
        / total
    )


def apply_inverse(flattened, inverse):
    return jnp.dot(
        flattened, inverse.T, precision=lax.Precision.HIGHEST, preferred_element_type=jnp.float32
    )


def _xor_pairs(n, bit):
    return [(i, i ^ bit) for i in range(n)]


def _power_of_two(n):
    return n > 0 and (n & (n - 1)) == 0


def reduce_gram(partial_value, hold=None):
    n_sub = lax.axis_size("sub")
    n_rows = lax.axis_size("rows")
    width = partial_value.shape[0]
    if not (_power_of_two(n_sub) and _power_of_two(n_rows) and n_sub >= 2 and width % 2 == 0):
        total = lax.psum(_gate(partial_value, hold or []), ("rows", "sub"))
        return total, total
    half = width // 2
    h = lax.axis_index("sub") % 2
    mine = lax.dynamic_slice_in_dim(partial_value, h * half, half, 0)
    theirs = lax.dynamic_slice_in_dim(partial_value, (1 - h) * half, half, 0)
    y = mine + lax.ppermute(theirs, "sub", _xor_pairs(n_sub, 1))
    bit = 2
    while bit < n_sub:
        y = y + lax.ppermute(y, "sub", _xor_pairs(n_sub, bit))
        bit *= 2
    if hold:
        y = jnp.where(_flag(hold), jnp.zeros_like(y), y)
    bit = 1
    while bit < n_rows:
        y = y + lax.ppermute(y, "rows", _xor_pairs(n_rows, bit))
        bit *= 2
    other = lax.ppermute(y, "sub", _xor_pairs(n_sub, 1))
    first_half = jnp.where(h == 0, y, other)
    second_half = jnp.where(h == 0, other, y)
    return jnp.concatenate([first_half, second_half], axis=0), y


def _flag(deps):
    flag = jnp.zeros((), jnp.bool_)
    for dep in deps:
        if dep is None:
            continue
        probe = dep[(0,) * dep.ndim]
        flag = flag | (probe != probe)
    return flag


def _gate(value, deps):
    flag = _flag(deps)
    corner = value[(slice(0, 1),) * value.ndim]
    kept = jnp.where(flag, jnp.zeros_like(corner), corner)
    return lax.dynamic_update_slice(value, kept, (0,) * value.ndim)


def per_device(held, held_block, held_count):
    capacity = held.shape[0]
    block_rows = held.shape[2]
    width = held.shape[3]
    devices_rows = lax.axis_size("rows")
    own_index = lax.axis_index("rows")
    per_slot = max(1, capacity // devices_rows)
    n_out = devices_rows * per_slot
    total = float(devices_rows * lax.axis_size("sub") * BLK_DEV * block_rows)
    blocks = held[:, 0]
    block_ids = held_block[:, 0]
    count = held_count[0, 0]
    slots = jnp.arange(capacity, dtype=jnp.int32)
    valid = slots < count

    def route(ids, filled):
        destination = ids // BLK_DEV
        earlier = (
            (destination[:, None] == destination[None, :])
            & filled[None, :]
            & (slots[None, :] < slots[:, None])
        )
        rank_within = jnp.sum(earlier.astype(jnp.int32), axis=1)
        return jnp.where(filled, destination * per_slot + rank_within, n_out)

    target = route(block_ids, valid)
    positions = jnp.arange(n_out, dtype=jnp.int32)
    match = target[None, :] == positions[:, None]
    source = jnp.sum(jnp.where(match, slots[None, :], 0), axis=1)
    source = source.reshape(devices_rows, per_slot)

    present = jnp.any(match, axis=1)
    labels = jnp.where(present, jnp.take(block_ids, jnp.sum(jnp.where(match, slots[None, :], 0), axis=1), mode="clip"), -1)
    labels = labels.reshape(devices_rows, per_slot).astype(jnp.float32)

    early = per_slot // 4
    middle = (per_slot - early) // 2
    bounds = [(0, early), (early, early + middle), (early + middle, per_slot)]

    def prepare(lo, hi, with_labels):
        if hi <= lo:
            return None
        chunk_source = source[:, lo:hi].reshape(-1)
        outgoing = jnp.take(blocks, chunk_source, axis=0, mode="clip")
        if with_labels:
            tile = jnp.zeros((devices_rows, 8, width), jnp.float32)
            tile = tile.at[:, 0, :per_slot].set(labels)
            outgoing = outgoing.reshape(devices_rows, (hi - lo) * block_rows, width)
            outgoing = jnp.concatenate([outgoing, tile], axis=1)
        return outgoing

    def send(lo, hi, outgoing, after, with_labels):
        if outgoing is None:
            return None, None
        if after is not None:
            outgoing = _gate(outgoing, [after])
        arrived = lax.all_to_all(outgoing, "rows", split_axis=0, concat_axis=0, tiled=True)
        if not with_labels:
            return arrived, None
        got = arrived[:, (hi - lo) * block_rows, :per_slot]
        data = arrived[:, : (hi - lo) * block_rows].reshape(-1, block_rows, width)
        return data, got

    def masked_gram(rows_of):
        kept = jnp.where(valid[:, None, None], rows_of.reshape(capacity, block_rows, width), 0.0)
        return (
            lax.dot_general(
                kept.reshape(-1, width),
                rows_of,
                (((0,), (0,)), ((), ())),
                precision=lax.Precision.HIGHEST,
                preferred_element_type=jnp.float32,
            )
            / total
        )

    arrived = [None, None, None]
    carrier = [k for k, (lo, hi) in enumerate(bounds) if hi > lo][-2:][0]
    outgoing = [prepare(lo, hi, carrier == k) for k, (lo, hi) in enumerate(bounds)]
    flat = blocks.reshape(-1, width)
    arrived[0], got0 = send(*bounds[0], outgoing[0], None, carrier == 0)
    gram_one = _gate(masked_gram(flat), [outgoing[1], outgoing[2]])
    reduced_one, rows_one = reduce_gram(gram_one, [arrived[0]])
    arrived[1], got1 = send(*bounds[1], outgoing[1], rows_one, carrier == 1)
    lower_one, inverse_one = factor(reduced_one)
    first_held = apply_inverse(flat, inverse_one)
    landed = got1 if carrier == 1 else arrived[1]
    reduced_two, rows_two = reduce_gram(masked_gram(first_held), [landed])
    arrived[2], got2 = send(*bounds[2], outgoing[2], rows_two, carrier == 2)
    lower_two, inverse_two = factor(reduced_two)
    arrived_labels = [got0, got1, got2][carrier].astype(jnp.int32)

    wanted = own_index * BLK_DEV + jnp.arange(BLK_DEV, dtype=jnp.int32)
    combined = _mm(inverse_one.T, inverse_two.T)
    resident = None
    for (lo, hi), chunk in zip(bounds, arrived):
        if chunk is None:
            continue
        chunk_labels = arrived_labels[:, lo:hi].reshape(-1)
        pick = (chunk_labels[None, :] == wanted[:, None]).astype(jnp.float32)
        if resident is not None and chunk is arrived[2]:
            pick = jnp.where(_flag([resident]), jnp.zeros_like(pick), pick)
        picked = lax.dot_general(
            pick,
            chunk,
            (((1,), (0,)), ((), ())),
            precision=lax.Precision.HIGHEST,
            preferred_element_type=jnp.float32,
        )
        resident = picked if resident is None else resident + picked
    resident = resident.reshape(-1, width)
    second = apply_inverse(resident, combined.T)
    result = second.reshape(BLK_DEV, block_rows, width)
    r_factor = jnp.dot(
        lower_two.T,
        lower_one.T,
        precision=lax.Precision.HIGHEST,
        preferred_element_type=jnp.float32,
    )
    return (result[:, None], r_factor)


def solution(mesh):
    in_specs = (P("rows", "sub", None, None), P("rows", "sub"), P("rows", "sub"))
    out_specs = (P("rows", "sub", None, None), P())
    return jax.shard_map(
        per_device, mesh=mesh, in_specs=in_specs, out_specs=out_specs, check_vma=False
    )
```
